256 devices in a mesh: row: 4 (over y), col: 16 (over z_hi, x, core), dep: 4 (over z_lo).
Axes of the slice: x: 4, y: 4, z: 8 (z_hi: 2, z_lo: 4; z = z_hi * 4 + z_lo), core: 2. Of those that a mesh axis runs over, the one named last changes fastest.
Arguments:
- grad_out: bfloat16 [4, 512, 12288], P('row', 'dep', 'col'), may hold values from -7 to 7
- out_weight: bfloat16 [8192, 12288], P('row', 'col'), may hold values from -0.09375 to 0.09375
- query_rows: bfloat16 [2048, 8192], P('dep', ('row', 'col')), may hold values from -6 to 6
- key_rows: bfloat16 [2048, 8192], P('dep', ('row', 'col')), may hold values from -6 to 6
- value_rows: bfloat16 [2048, 8192], P('dep', ('row', 'col')), may hold values from -7 to 7
- seg_lengths: int32 [8], replicated, may hold values from 1 to 1536, 2048 in all
Outputs:
- grad_weight: float32 [8192, 12288], P('row', 'col')
- grad_query: bfloat16 [2048, 8192], P('dep', ('row', 'col'))
- grad_key: bfloat16 [2048, 8192], P('dep', ('row', 'col'))
- grad_value: bfloat16 [2048, 8192], P('dep', ('row', 'col'))
The draws below stay inside these ranges and needn't reach their ends.
All inputs are finite; a program needn't handle non-finite values.
Results may differ from the reference program's by a relative error of at most 0.029.
Values may be sent and summed in bfloat16 or wider, within the bound.
No kernel may reach another device: no remote copies, remote signals or barrier semaphores. Data moves between devices by JAX's collectives and lax.ppermute only.
A program may use at most 128 MiB of HBM per device.

```python
import math
from functools import partial
import jax
import jax.numpy as jnp
import numpy as np
from jax import lax

D = 12288
HD = 128
HEADS = 64
HH = 8192
TOK_DEV = 128
TOKENS = 2048
SEGS = 8
MOST = 1536
N_ROW = 4
N_DEP = 4


def query_key_pair(key):
    base_key = jax.random.fold_in(key, 17)
    first_key, second_key = jax.random.split(base_key, 2)
    grid_shape = (TOKENS, HH)
    query_draw = jnp.clip(2.0 * jax.random.normal(first_key, grid_shape, jnp.float32), -6.0, 6.0)
    key_draw = jnp.clip(2.0 * jax.random.normal(second_key, grid_shape, jnp.float32), -6.0, 6.0)
    return (query_draw, key_draw)


def draw_query_rows(key, part):
    return query_key_pair(key)[0].astype(jnp.bfloat16)


def draw_key_rows(key, part):
    return query_key_pair(key)[1].astype(jnp.bfloat16)


def draw_grad_out(key, part):
    noise_key = jax.random.fold_in(jax.random.fold_in(key, 31), 0)
    grid_shape = (N_ROW, TOKENS // N_ROW, D)
    field = jnp.clip(jax.random.normal(noise_key, grid_shape, jnp.float32), -4.0, 4.0)
    return field.astype(jnp.bfloat16)


def draw_value_rows(key, part):
    noise_key = jax.random.fold_in(key, 47)
    grid_shape = (TOKENS, HH)
    field = 0.9 * jnp.clip(jax.random.normal(noise_key, grid_shape, jnp.float32), -4.0, 4.0)
    return field.astype(jnp.bfloat16)


def spiked(result, key, source, target, parts, factor):
    owner, partner = [(jnp.arange(result.shape[axis_at]) // (result.shape[axis_at] // parts)).reshape([-1 if axis == axis_at else 1 for axis in range(result.ndim)]) for axis_at in (source, target)]
    chosen = jax.random.permutation(key, parts)[partner]
    strong = (owner == chosen) | (owner == (partner + parts // 2) % parts)
    return jnp.where(strong, factor * result, result)


def steps_of(own_key, dims, cuts, smallest, top_value):
    def one(axis_at, blocks):
        draws = jax.random.uniform(jax.random.fold_in(jax.random.fold_in(own_key, 6), axis_at), (blocks,), jnp.float32, smallest / len(cuts), top_value / len(cuts))
        return jnp.repeat(jnp.exp(draws), dims[axis_at] // blocks).reshape((-1,) + (1,) * (len(dims) - axis_at - 1))

    gain = one(*cuts[0])
    for cut in cuts[1:]:
        gain = gain * one(*cut)
    return gain


def profile(number_of, total, most, slope):
    portions = [(1 << 20) // math.isqrt(grade ** slope) + 1 for grade in range(2, number_of + 1)]
    rest, holding = total - most - (number_of - 1), [1] * (number_of - 1)
    while rest > 0:
        candidates = [i for i in range(number_of - 1) if holding[i] < most]
        mass, budget = sum([portions[i] for i in candidates]), rest
        for i in candidates:
            addition = min(most - holding[i], max(1, budget * portions[i] // mass), rest)
            holding[i] = holding[i] + addition
            rest = rest - addition
    return np.array([most] + holding)


def ragged_sizes(own_key, amount, total, reach, skew):
    if amount == 2:
        one = jax.random.randint(own_key, (), max(1, total - reach), min(reach, total - 1) + 1)
        return jnp.stack([one, total - one])
    lengths = jnp.asarray(profile(amount, total, reach, skew), jnp.int32)
    couples = (amount - 1) // 2
    source_of, sink = lengths[1:1 + 2 * couples:2], lengths[2:2 + 2 * couples:2]
    margin = jnp.minimum(source_of - 1, reach - sink)
    shifted = jax.random.randint(jax.random.fold_in(own_key, 1), (couples,), 0, 1 << 20) % (margin + 1)
    lengths = lengths.at[1:1 + 2 * couples:2].set(source_of - shifted).at[2:2 + 2 * couples:2].set(sink + shifted)
    return lengths[jax.random.permutation(jax.random.fold_in(own_key, 2), amount)]


def bell_draw_with(own_key, dims, scale, most, shards, heavy, held_as=jnp.bfloat16):
    array = scale * jax.random.normal(own_key, dims, jnp.float32)
    if shards:
        array = array * steps_of(own_key, dims, shards, -0.22, 0.18)
    return jnp.clip(spiked(array, jax.random.fold_in(own_key, 3), *heavy), -most, most).astype(held_as)


def setup_inputs(seed: int = 0) -> dict:
    keys = jax.random.split(jax.random.key(seed), 7)
    return {
        "grad_out": draw_grad_out(jax.random.fold_in(keys[6], 71), 0),
        "out_weight": bell_draw_with(keys[1], (HH, D), HH ** -0.5, 0.09375, ((0, 4), (1, 16)), (1, 0, 16, 2.0)),
        "query_rows": draw_query_rows(jax.random.fold_in(keys[6], 71), 0),
        "key_rows": draw_key_rows(jax.random.fold_in(keys[6], 71), 0),
        "value_rows": draw_value_rows(jax.random.fold_in(keys[6], 71), 0),
        "seg_lengths": ragged_sizes(keys[5], SEGS, TOKENS, MOST, 2).astype(jnp.int32),
    }


NEG_FILL = -1e+30

def segment_of(seg_lengths, positions):
    seg_ends = jnp.cumsum(seg_lengths).astype(jnp.int32)
    return lax.optimization_barrier(jnp.sum((positions[:, None] >= seg_ends[None, :]).astype(jnp.int32), axis=1))

def attend_head(inputs, allowed, inv_root):
    q_head, k_head, v_head, grad_head = inputs
    scores = jnp.dot(q_head, k_head.T, preferred_element_type=jnp.float32) * inv_root
    masked = jnp.where(allowed, scores, NEG_FILL)
    row_max = lax.optimization_barrier(jnp.max(masked, axis=1, keepdims=True))
    exponent = jnp.where(allowed, jnp.exp(masked - row_max), 0.0)
    prob_full = exponent / lax.optimization_barrier(jnp.sum(exponent, axis=1, keepdims=True))
    prob_half = prob_full.astype(jnp.bfloat16)
    context = jnp.dot(prob_half, v_head, preferred_element_type=jnp.float32).astype(jnp.bfloat16)
    grad_prob = jnp.dot(grad_head, v_head.T, preferred_element_type=jnp.float32)
    delta_row = lax.optimization_barrier(jnp.sum(prob_full * grad_prob, axis=1, keepdims=True))
    grad_score = (prob_full * (grad_prob - delta_row)).astype(jnp.bfloat16)
    grad_q = (jnp.dot(grad_score, k_head, preferred_element_type=jnp.float32) * inv_root).astype(jnp.bfloat16)
    grad_k = (jnp.dot(grad_score.T, q_head, preferred_element_type=jnp.float32) * inv_root).astype(jnp.bfloat16)
    grad_v = jnp.dot(prob_half.T, grad_head, preferred_element_type=jnp.float32).astype(jnp.bfloat16)
    return (context, grad_q, grad_k, grad_v)

def split_heads(matrix):
    return matrix.reshape(TOKENS, HEADS, HD).transpose(1, 0, 2)

def merge_heads(stacked):
    return stacked.transpose(1, 0, 2).reshape(TOKENS, HEADS * HD)

def reference(grad_out, out_weight, query_rows, key_rows, value_rows, seg_lengths):
    grad_rows = grad_out.reshape(N_ROW, N_DEP, TOK_DEV, D).transpose(1, 0, 2, 3).reshape(TOKENS, D)
    positions = jnp.arange(TOKENS, dtype=jnp.int32)
    segment = segment_of(seg_lengths, positions)
    allowed = (segment[:, None] == segment[None, :]) & (positions[None, :] <= positions[:, None])
    context_grad = jnp.dot(grad_rows, out_weight.T, preferred_element_type=jnp.float32).astype(jnp.bfloat16)
    inv_root = 1.0 / math.sqrt(HD)
    results = lax.map(partial(attend_head, allowed=allowed, inv_root=inv_root), (split_heads(query_rows), split_heads(key_rows), split_heads(value_rows), split_heads(context_grad)))
    context = merge_heads(results[0])
    grad_weight = jnp.zeros((HEADS * HD, D), jnp.float32)
    depth_rows = N_ROW * TOK_DEV
    for depth in range(N_DEP):
        ctx_part = lax.slice_in_dim(context, depth * depth_rows, (depth + 1) * depth_rows, axis=0)
        grad_part = lax.slice_in_dim(grad_rows, depth * depth_rows, (depth + 1) * depth_rows, axis=0)
        piece = jnp.dot(ctx_part.T, grad_part, preferred_element_type=jnp.float32)
        grad_weight = grad_weight + lax.optimization_barrier(piece.astype(jnp.bfloat16)).astype(jnp.float32)
    return (grad_weight, merge_heads(results[1]), merge_heads(results[2]), merge_heads(results[3]))
```

```python
import math

import jax
import jax.numpy as jnp
from jax import lax
from jax.sharding import Mesh
from jax.sharding import PartitionSpec as P

NEG_FILL = -1e30
COL = ("zh", "x", "core")
DEP = "zl"


def segment_count(positions, seg_ends):
    return jnp.sum((positions[:, None] >= seg_ends[None, :]).astype(jnp.int32), axis=1)


def shift(x, axis, n, s):
    return lax.ppermute(x, axis, [(i, (i + s) % n) for i in range(n)])


def pp_gather(x, axis, n):
    me = lax.axis_index(axis)
    parts = [x] + [shift(x, axis, n, -s) for s in range(1, n)]
    return jnp.roll(jnp.concatenate(parts, 0), me, axis=0)


def pp_reduce_scatter(x, axis, n):
    me = lax.axis_index(axis)
    acc = jnp.take(x, me, axis=0).astype(jnp.float32)
    for s in range(1, n):
        send = jnp.take(x, (me + s) % n, axis=0)
        acc = acc + shift(send, axis, n, s).astype(jnp.float32)
    return acc


def make_shards(n_zh, n_x, n_core, n_row, n_dep):
    def shards(grad_out, out_weight, query_rows, key_rows, value_rows, seg_lengths):
        n_tok, feat = grad_out.shape[1], grad_out.shape[2]
        tok_depth = n_row * n_tok
        head_dim = query_rows.shape[1]
        inv_root = 1.0 / math.sqrt(head_dim)

        rows_all = lax.all_gather(
            lax.all_gather(grad_out, DEP, axis=1, tiled=True), "row", axis=0, tiled=True
        ).reshape(n_row, n_dep, n_tok, feat)

        grad_rows = pp_gather(grad_out, "row", n_row).reshape(tok_depth, feat)
        partial = jnp.einsum(
            "hf,tf->ht", out_weight, grad_rows, preferred_element_type=jnp.float32
        ).astype(jnp.bfloat16)
        partial = partial.reshape(n_zh, n_x, n_core, head_dim, tok_depth)
        partial = jnp.transpose(partial, (2, 0, 1, 3, 4))
        partial = pp_reduce_scatter(partial, "core", n_core).astype(jnp.bfloat16)
        partial = jnp.transpose(partial, (1, 0, 2, 3))
        partial = pp_reduce_scatter(partial, "x", n_x).astype(jnp.bfloat16)
        context_grad = pp_reduce_scatter(partial, "zh", n_zh).astype(jnp.bfloat16).T

        kv = jnp.concatenate([key_rows, value_rows], axis=1)[None]
        kv_all = pp_gather(kv, DEP, n_dep).reshape(n_dep * tok_depth, 2 * head_dim)
        keys_all, values_all = kv_all[:, :head_dim], kv_all[:, head_dim:]
        key_total = keys_all.shape[0]
        seg_ends = jnp.cumsum(seg_lengths)
        key_pos = jnp.arange(key_total, dtype=jnp.int32)
        key_seg = segment_count(key_pos, seg_ends)
        query_pos = lax.axis_index(DEP) * tok_depth + jnp.arange(tok_depth, dtype=jnp.int32)
        query_seg = segment_count(query_pos, seg_ends)
        allowed = (query_seg[:, None] == key_seg[None, :]) & (
            key_pos[None, :] <= query_pos[:, None]
        )
        scores = (
            jnp.einsum("qh,kh->qk", query_rows, keys_all, preferred_element_type=jnp.float32)
            * inv_root
        )
        masked = jnp.where(allowed, scores, NEG_FILL)
        row_max = jnp.max(masked, axis=1, keepdims=True)
        exponent = jnp.where(allowed, jnp.exp(masked - row_max), 0.0)
        row_sum = jnp.sum(exponent, axis=1, keepdims=True)
        prob_full = exponent / row_sum
        prob_half = prob_full.astype(jnp.bfloat16)
        context = jnp.dot(prob_half, values_all, preferred_element_type=jnp.float32).astype(
            jnp.bfloat16
        )
        ctx_all = lax.all_gather(context[None], ("zh", DEP, "x", "core"), axis=0, tiled=True)
        ctx_all = ctx_all.reshape(n_zh, n_dep, n_x, n_core, tok_depth, head_dim)

        grad_prob = jnp.dot(context_grad, values_all.T, preferred_element_type=jnp.float32)
        delta_row = jnp.sum(prob_full * grad_prob, axis=1, keepdims=True)
        grad_score = (prob_full * (grad_prob - delta_row)).astype(jnp.bfloat16)
        grad_query = (
            jnp.dot(grad_score, keys_all, preferred_element_type=jnp.float32) * inv_root
        ).astype(jnp.bfloat16)
        key_partial = (
            jnp.einsum("qk,qh->kh", grad_score, query_rows, preferred_element_type=jnp.float32)
            * inv_root
        ).astype(jnp.bfloat16)
        value_partial = jnp.einsum(
            "qk,qh->kh", prob_half, context_grad, preferred_element_type=jnp.float32
        ).astype(jnp.bfloat16)
        kv_partial = jnp.concatenate([key_partial, value_partial], axis=1)
        kv_grad = pp_reduce_scatter(
            kv_partial.reshape(n_dep, tok_depth, 2 * head_dim), DEP, n_dep
        ).astype(jnp.bfloat16)
        grad_key, grad_value = kv_grad[:, :head_dim], kv_grad[:, head_dim:]

        grad_weight = jnp.zeros((n_zh, n_x, n_core, head_dim, feat), jnp.float32)
        for depth in range(n_dep):
            rows_depth = rows_all[:, depth].reshape(tok_depth, feat)
            piece = jnp.einsum(
                "zxcth,tf->zxchf",
                ctx_all[:, depth],
                rows_depth,
                preferred_element_type=jnp.float32,
            )
            grad_weight = grad_weight + lax.optimization_barrier(
                piece.astype(jnp.bfloat16)
            ).astype(jnp.float32)
        grad_weight = grad_weight.reshape(n_zh * n_x * n_core * head_dim, feat)
        return (grad_weight, grad_query, grad_key, grad_value)

    return shards


def solution(mesh):
    n_row, n_col, n_dep = mesh.shape["row"], mesh.shape["col"], mesh.shape["dep"]
    n_zh, n_core = 2, 2
    n_x = n_col // (n_zh * n_core)
    fine = Mesh(
        mesh.devices.reshape(n_row, n_zh, n_x, n_core, n_dep), ("row",) + COL + (DEP,)
    )
    in_specs = (
        P("row", DEP, COL),
        P("row", COL),
        P(DEP, ("row",) + COL),
        P(DEP, ("row",) + COL),
        P(DEP, ("row",) + COL),
        P(),
    )
    out_specs = (
        P("row", COL),
        P(DEP, ("row",) + COL),
        P(DEP, ("row",) + COL),
        P(DEP, ("row",) + COL),
    )
    return jax.shard_map(
        make_shards(n_zh, n_x, n_core, n_row, n_dep),
        mesh=fine,
        in_specs=in_specs,
        out_specs=out_specs,
        check_vma=False,
    )
```

```python
import math

import jax
import jax.numpy as jnp
from jax import lax
from jax.sharding import Mesh
from jax.sharding import PartitionSpec as P

NEG_FILL = -1e30
FAR = 1 << 30
COL = ("zh", "x", "core")
DEP = "zl"


def segment_count(positions, seg_ends):
    return jnp.sum((positions[:, None] >= seg_ends[None, :]).astype(jnp.int32), axis=1)


def shift(x, axis, n, s):
    return lax.ppermute(x, axis, [(i, (i + s) % n) for i in range(n)])


def shift_open(x, axis, n, s):
    return lax.ppermute(x, axis, [(i, i + s) for i in range(n) if 0 <= i + s < n])


def roll_rows(x, amount, axis):
    size = x.shape[axis]
    doubled = jnp.concatenate([x, x], axis=axis)
    return lax.dynamic_slice_in_dim(doubled, (size - amount) % size, size, axis=axis)


def rolled_gather(x, axis, n, stack_axis=0):
    parts = [x] + [shift(x, axis, n, -s) for s in range(1, n)]
    return jnp.stack(parts, axis=stack_axis)


def pp_reduce_scatter(x, axis, n, dim):
    me = lax.axis_index(axis)
    acc = lax.dynamic_index_in_dim(x, me, dim, keepdims=False).astype(jnp.float32)
    for s in range(1, n):
        send = lax.dynamic_index_in_dim(x, (me + s) % n, dim, keepdims=False)
        acc = acc + shift(send, axis, n, s).astype(jnp.float32)
    return acc


def make_shards(n_zh, n_x, n_core, n_row, n_dep):
    def shards(grad_out, out_weight, query_rows, key_rows, value_rows, seg_lengths):
        n_tok, feat = grad_out.shape[1], grad_out.shape[2]
        tok_depth = n_row * n_tok
        head_dim = query_rows.shape[1]
        inv_root = 1.0 / math.sqrt(head_dim)
        me_r = lax.axis_index("row")
        me_d = lax.axis_index(DEP)
        local = grad_out[0]

        grad_rows = rolled_gather(local, "row", n_row).reshape(tok_depth, feat)
        partial = jnp.einsum(
            "hf,tf->ht", out_weight, grad_rows, preferred_element_type=jnp.float32
        ).astype(jnp.bfloat16)
        partial = partial.reshape(n_zh, n_x, n_core, head_dim, tok_depth)
        partial = pp_reduce_scatter(partial, "core", n_core, 2).astype(jnp.bfloat16)
        partial = pp_reduce_scatter(partial, "x", n_x, 1).astype(jnp.bfloat16)
        partial = pp_reduce_scatter(partial, "zh", n_zh, 0).astype(jnp.bfloat16)
        context_grad = roll_rows(partial.T, me_r * n_tok, 0)

        kv = jnp.concatenate([key_rows, value_rows], axis=1)
        kv_all = jnp.stack(
            [kv] + [shift_open(kv, DEP, n_dep, s) for s in range(1, n_dep)], axis=0
        ).reshape(n_dep * tok_depth, 2 * head_dim)
        keys_all, values_all = kv_all[:, :head_dim], kv_all[:, head_dim:]
        src_depth = me_d - jnp.arange(n_dep, dtype=jnp.int32)
        key_pos = (
            jnp.where(src_depth >= 0, src_depth * tok_depth, FAR)[:, None]
            + jnp.arange(tok_depth, dtype=jnp.int32)[None, :]
        ).reshape(-1)
        seg_ends = jnp.cumsum(seg_lengths)
        key_seg = segment_count(key_pos, seg_ends)
        query_pos = me_d * tok_depth + jnp.arange(tok_depth, dtype=jnp.int32)
        query_seg = segment_count(query_pos, seg_ends)
        allowed = (query_seg[:, None] == key_seg[None, :]) & (
            key_pos[None, :] <= query_pos[:, None]
        )
        scores = (
            jnp.einsum("qh,kh->qk", query_rows, keys_all, preferred_element_type=jnp.float32)
            * inv_root
        )
        masked = jnp.where(allowed, scores, NEG_FILL)
        row_max = jnp.max(masked, axis=1, keepdims=True)
        exponent = jnp.where(allowed, jnp.exp(masked - row_max), 0.0)
        row_sum = jnp.sum(exponent, axis=1, keepdims=True)
        prob_full = exponent / row_sum
        prob_half = prob_full.astype(jnp.bfloat16)
        context = jnp.dot(prob_half, values_all, preferred_element_type=jnp.float32).astype(
            jnp.bfloat16
        )
        context = roll_rows(context, -me_r * n_tok, 0)
        ctx_all = lax.all_gather(context[None], COL + (DEP,), axis=0, tiled=True)
        ctx_all = ctx_all.reshape(n_zh * n_x * n_core, n_dep * tok_depth, head_dim)

        grad_prob = jnp.dot(context_grad, values_all.T, preferred_element_type=jnp.float32)
        delta_row = jnp.sum(prob_full * grad_prob, axis=1, keepdims=True)
        grad_score = (prob_full * (grad_prob - delta_row)).astype(jnp.bfloat16)
        grad_query = (
            jnp.dot(grad_score, keys_all, preferred_element_type=jnp.float32) * inv_root
        ).astype(jnp.bfloat16)
        key_partial = (
            jnp.einsum("qk,qh->kh", grad_score, query_rows, preferred_element_type=jnp.float32)
            * inv_root
        ).astype(jnp.bfloat16)
        value_partial = jnp.einsum(
            "qk,qh->kh", prob_half, context_grad, preferred_element_type=jnp.float32
        ).astype(jnp.bfloat16)
        kv_partial = jnp.concatenate([key_partial, value_partial], axis=1).reshape(
            n_dep, tok_depth, 2 * head_dim
        )
        kv_grad = kv_partial[0].astype(jnp.float32)
        for s in range(1, n_dep):
            kv_grad = kv_grad + shift_open(kv_partial[s], DEP, n_dep, -s).astype(jnp.float32)
        kv_grad = kv_grad.astype(jnp.bfloat16)
        grad_key, grad_value = kv_grad[:, :head_dim], kv_grad[:, head_dim:]

        by_depth = roll_rows(rolled_gather(local, DEP, n_dep), me_d, 0)
        rows_all = rolled_gather(by_depth, "row", n_row, stack_axis=1)
        rows_all = rows_all.reshape(n_dep * tok_depth, feat)
        grad_weight = jnp.einsum(
            "ntk,tf->nkf", ctx_all, rows_all, preferred_element_type=jnp.float32
        ).reshape(n_zh * n_x * n_core * head_dim, feat)
        return (grad_weight, grad_query, grad_key, grad_value)

    return shards


def solution(mesh):
    n_row, n_col, n_dep = mesh.shape["row"], mesh.shape["col"], mesh.shape["dep"]
    n_zh, n_core = 2, 2
    n_x = n_col // (n_zh * n_core)
    fine = Mesh(
        mesh.devices.reshape(n_row, n_zh, n_x, n_core, n_dep), ("row",) + COL + (DEP,)
    )
    in_specs = (
        P("row", DEP, COL),
        P("row", COL),
        P(DEP, ("row",) + COL),
        P(DEP, ("row",) + COL),
        P(DEP, ("row",) + COL),
        P(),
    )
    out_specs = (
        P("row", COL),
        P(DEP, ("row",) + COL),
        P(DEP, ("row",) + COL),
        P(DEP, ("row",) + COL),
    )
    return jax.shard_map(
        make_shards(n_zh, n_x, n_core, n_row, n_dep),
        mesh=fine,
        in_specs=in_specs,
        out_specs=out_specs,
        check_vma=False,
    )
```

```python
import math

import jax
import jax.numpy as jnp
from jax import lax
from jax.sharding import Mesh
from jax.sharding import PartitionSpec as P

NEG_FILL = -1e30
FAR = 1 << 30
COL = ("zh", "x", "core")
DEP = "zl"


def segment_count(positions, seg_ends):
    return jnp.sum((positions[:, None] >= seg_ends[None, :]).astype(jnp.int32), axis=1)


def shift(x, axis, n, s):
    return lax.ppermute(x, axis, [(i, (i + s) % n) for i in range(n)])


def shift_open(x, axis, n, s):
    return lax.ppermute(x, axis, [(i, i + s) for i in range(n) if 0 <= i + s < n])


def roll_rows(x, amount, axis):
    size = x.shape[axis]
    doubled = jnp.concatenate([x, x], axis=axis)
    return lax.dynamic_slice_in_dim(doubled, (size - amount) % size, size, axis=axis)


def rolled_gather(x, axis, n, stack_axis=0):
    parts = [x] + [shift(x, axis, n, -s) for s in range(1, n)]
    return jnp.stack(parts, axis=stack_axis)


def pp_reduce_scatter(x, axis, n, dim):
    me = lax.axis_index(axis)
    acc = lax.dynamic_index_in_dim(x, me, dim, keepdims=False).astype(jnp.float32)
    for s in range(1, n):
        send = lax.dynamic_index_in_dim(x, (me + s) % n, dim, keepdims=False)
        acc = acc + shift(send, axis, n, s).astype(jnp.float32)
    return acc


def make_shards(n_zh, n_x, n_core, n_row, n_dep):
    def shards(grad_out, out_weight, query_rows, key_rows, value_rows, seg_lengths):
        n_tok, feat = grad_out.shape[1], grad_out.shape[2]
        tok_depth = n_row * n_tok
        head_dim = query_rows.shape[1]
        inv_root = 1.0 / math.sqrt(head_dim)
        me_r = lax.axis_index("row")
        me_d = lax.axis_index(DEP)
        local = grad_out[0]

        grad_rows = rolled_gather(local, "row", n_row).reshape(tok_depth, feat)
        partial = jnp.einsum(
            "tf,hf->th", grad_rows, out_weight, preferred_element_type=jnp.float32
        ).astype(jnp.bfloat16)
        partial = partial.reshape(tok_depth, n_zh, n_x, n_core, head_dim)
        partial = pp_reduce_scatter(partial, "core", n_core, 3).astype(jnp.bfloat16)
        partial = pp_reduce_scatter(partial, "x", n_x, 2).astype(jnp.bfloat16)
        partial = pp_reduce_scatter(partial, "zh", n_zh, 1).astype(jnp.bfloat16)
        context_grad = roll_rows(partial, me_r * n_tok, 0)

        kv = jnp.concatenate([key_rows, value_rows], axis=1)
        kv_all = jnp.stack(
            [kv] + [shift_open(kv, DEP, n_dep, s) for s in range(1, n_dep)], axis=0
        ).reshape(n_dep * tok_depth, 2 * head_dim)
        keys_all, values_all = kv_all[:, :head_dim], kv_all[:, head_dim:]
        src_depth = me_d - jnp.arange(n_dep, dtype=jnp.int32)
        key_pos = (
            jnp.where(src_depth >= 0, src_depth * tok_depth, FAR)[:, None]
            + jnp.arange(tok_depth, dtype=jnp.int32)[None, :]
        ).reshape(-1)
        seg_ends = jnp.cumsum(seg_lengths)
        key_seg = segment_count(key_pos, seg_ends)
        query_pos = me_d * tok_depth + jnp.arange(tok_depth, dtype=jnp.int32)
        query_seg = segment_count(query_pos, seg_ends)
        allowed = (query_seg[:, None] == key_seg[None, :]) & (
            key_pos[None, :] <= query_pos[:, None]
        )
        scores = (
            jnp.einsum("qh,kh->qk", query_rows, keys_all, preferred_element_type=jnp.float32)
            * inv_root
        )
        masked = jnp.where(allowed, scores, NEG_FILL)
        row_max = jnp.max(masked, axis=1, keepdims=True)
        exponent = jnp.where(allowed, jnp.exp(masked - row_max), 0.0)
        row_sum = jnp.sum(exponent, axis=1, keepdims=True)
        prob_full = exponent / row_sum
        prob_half = prob_full.astype(jnp.bfloat16)
        context = jnp.dot(prob_half, values_all, preferred_element_type=jnp.float32).astype(
            jnp.bfloat16
        )
        by_depth = roll_rows(rolled_gather(local, DEP, n_dep), me_d, 0)
        rows_all = rolled_gather(by_depth, "row", n_row, stack_axis=1)
        context = roll_rows(context, -me_r * n_tok, 0)
        context, rows_all = lax.optimization_barrier((context, rows_all))
        ctx_all = lax.all_gather(context[None], ("zh", DEP, "x", "core"), axis=0, tiled=True)
        ctx_all = ctx_all.reshape(n_zh, n_dep, n_x, n_core, tok_depth, head_dim)

        grad_prob = jnp.dot(context_grad, values_all.T, preferred_element_type=jnp.float32)
        delta_row = jnp.sum(prob_full * grad_prob, axis=1, keepdims=True)
        grad_score = (prob_full * (grad_prob - delta_row)).astype(jnp.bfloat16)
        grad_query = (
            jnp.dot(grad_score, keys_all, preferred_element_type=jnp.float32) * inv_root
        ).astype(jnp.bfloat16)
        key_partial = (
            jnp.einsum("qk,qh->kh", grad_score, query_rows, preferred_element_type=jnp.float32)
            * inv_root
        ).astype(jnp.bfloat16)
        value_partial = jnp.einsum(
            "qk,qh->kh", prob_half, context_grad, preferred_element_type=jnp.float32
        ).astype(jnp.bfloat16)
        kv_partial = jnp.concatenate([key_partial, value_partial], axis=1).reshape(
            n_dep, tok_depth, 2 * head_dim
        )
        kv_grad = kv_partial[0].astype(jnp.float32)
        for s in range(1, n_dep):
            kv_grad = kv_grad + shift_open(kv_partial[s], DEP, n_dep, -s).astype(jnp.float32)
        kv_grad = kv_grad.astype(jnp.bfloat16)
        grad_key, grad_value = kv_grad[:, :head_dim], kv_grad[:, head_dim:]

        grad_weight = None
        for depth in range(n_dep):
            piece = jnp.einsum(
                "zxcth,tf->zxchf",
                ctx_all[:, depth],
                rows_all[depth].reshape(tok_depth, feat),
                preferred_element_type=jnp.float32,
            )
            grad_weight = piece if grad_weight is None else grad_weight + piece
        grad_weight = grad_weight.reshape(n_zh * n_x * n_core * head_dim, feat)
        return (grad_weight, grad_query, grad_key, grad_value)

    return shards


def solution(mesh):
    n_row, n_col, n_dep = mesh.shape["row"], mesh.shape["col"], mesh.shape["dep"]
    n_zh, n_core = 2, 2
    n_x = n_col // (n_zh * n_core)
    fine = Mesh(
        mesh.devices.reshape(n_row, n_zh, n_x, n_core, n_dep), ("row",) + COL + (DEP,)
    )
    in_specs = (
        P("row", DEP, COL),
        P("row", COL),
        P(DEP, ("row",) + COL),
        P(DEP, ("row",) + COL),
        P(DEP, ("row",) + COL),
        P(),
    )
    out_specs = (
        P("row", COL),
        P(DEP, ("row",) + COL),
        P(DEP, ("row",) + COL),
        P(DEP, ("row",) + COL),
    )
    return jax.shard_map(
        make_shards(n_zh, n_x, n_core, n_row, n_dep),
        mesh=fine,
        in_specs=in_specs,
        out_specs=out_specs,
        check_vma=False,
    )
```

```python
import math

import jax
import jax.numpy as jnp
from jax import lax
from jax.sharding import Mesh
from jax.sharding import PartitionSpec as P

NEG_FILL = -1e30
COL = ("zh", "x", "core")
DEP = "zl"


def segment_count(positions, seg_ends):
    return jnp.sum((positions[:, None] >= seg_ends[None, :]).astype(jnp.int32), axis=1)


def shift(x, axis, n, s):
    return lax.ppermute(x, axis, [(i, (i + s) % n) for i in range(n)])


def roll_rows(x, amount, axis):
    size = x.shape[axis]
    doubled = jnp.concatenate([x, x], axis=axis)
    return lax.dynamic_slice_in_dim(doubled, (size - amount) % size, size, axis=axis)


def rolled_gather(x, axis, n, stack_axis=0):
    parts = [x] + [shift(x, axis, n, -s) for s in range(1, n)]
    return jnp.stack(parts, axis=stack_axis)


def pp_reduce_scatter(x, axis, n, dim):
    me = lax.axis_index(axis)
    acc = lax.dynamic_index_in_dim(x, me, dim, keepdims=False).astype(jnp.float32)
    for s in range(1, n):
        send = lax.dynamic_index_in_dim(x, (me + s) % n, dim, keepdims=False)
        acc = acc + shift(send, axis, n, s).astype(jnp.float32)
    return acc


def make_shards(n_zh, n_x, n_core, n_row, n_dep):
    def shards(grad_out, out_weight, query_rows, key_rows, value_rows, seg_lengths):
        n_tok, feat = grad_out.shape[1], grad_out.shape[2]
        tok_depth = n_row * n_tok
        head_dim = query_rows.shape[1]
        inv_root = 1.0 / math.sqrt(head_dim)
        me_r = lax.axis_index("row")
        me_d = lax.axis_index(DEP)
        local = grad_out[0]

        kv = jnp.concatenate([key_rows, value_rows], axis=1)
        packed = jnp.concatenate([kv, local.reshape(-1, 2 * head_dim)], axis=0)
        packed_all = rolled_gather(packed, DEP, n_dep)
        kv_all = packed_all[:, :tok_depth].reshape(n_dep * tok_depth, 2 * head_dim)
        keys_all, values_all = kv_all[:, :head_dim], kv_all[:, head_dim:]
        by_depth = roll_rows(packed_all[:, tok_depth:].reshape(n_dep, n_tok, feat), me_d, 0)

        src_depth = (me_d + jnp.arange(n_dep, dtype=jnp.int32)) % n_dep
        key_pos = (
            (src_depth * tok_depth)[:, None] + jnp.arange(tok_depth, dtype=jnp.int32)[None, :]
        ).reshape(-1)
        seg_ends = jnp.cumsum(seg_lengths)
        key_seg = segment_count(key_pos, seg_ends)
        query_pos = me_d * tok_depth + jnp.arange(tok_depth, dtype=jnp.int32)
        query_seg = segment_count(query_pos, seg_ends)
        allowed = (query_seg[:, None] == key_seg[None, :]) & (
            key_pos[None, :] <= query_pos[:, None]
        )
        scores = (
            jnp.einsum("qh,kh->qk", query_rows, keys_all, preferred_element_type=jnp.float32)
            * inv_root
        )
        masked = jnp.where(allowed, scores, NEG_FILL)
        row_max = jnp.max(masked, axis=1, keepdims=True)
        exponent = jnp.where(allowed, jnp.exp(masked - row_max), 0.0)
        row_sum = jnp.sum(exponent, axis=1, keepdims=True)
        prob_full = exponent / row_sum
        prob_half = prob_full.astype(jnp.bfloat16)
        context = jnp.dot(prob_half, values_all, preferred_element_type=jnp.float32).astype(
            jnp.bfloat16
        )

        rows_all = rolled_gather(by_depth, "row", n_row, stack_axis=1)
        context = roll_rows(context, -me_r * n_tok, 0)
        context, rows_all = lax.optimization_barrier((context, rows_all))
        ctx_all = lax.all_gather(context[None], ("zh", DEP, "x", "core"), axis=0, tiled=True)
        ctx_all = ctx_all.reshape(n_zh, n_dep, n_x, n_core, tok_depth, head_dim)

        weight_perm = jnp.transpose(
            out_weight.reshape(n_zh, n_x, n_core, head_dim, feat), (2, 1, 0, 3, 4)
        ).reshape(-1, feat)
        grad_rows = lax.dynamic_index_in_dim(rows_all, me_d, 0, keepdims=False)
        partial = jnp.einsum(
            "tf,hf->th",
            grad_rows.reshape(tok_depth, feat),
            weight_perm,
            preferred_element_type=jnp.float32,
        ).astype(jnp.bfloat16)
        partial = pp_reduce_scatter(
            partial.reshape(tok_depth, n_core, -1), "core", n_core, 1
        ).astype(jnp.bfloat16)
        partial = pp_reduce_scatter(partial.reshape(tok_depth, n_x, -1), "x", n_x, 1).astype(
            jnp.bfloat16
        )
        partial = pp_reduce_scatter(
            partial.reshape(tok_depth, n_zh, -1), "zh", n_zh, 1
        ).astype(jnp.bfloat16)
        context_grad = roll_rows(partial, me_r * n_tok, 0)

        grad_prob = jnp.dot(context_grad, values_all.T, preferred_element_type=jnp.float32)
        delta_row = jnp.sum(prob_full * grad_prob, axis=1, keepdims=True)
        grad_score = (prob_full * (grad_prob - delta_row)).astype(jnp.bfloat16)
        grad_query = (
            jnp.dot(grad_score, keys_all, preferred_element_type=jnp.float32) * inv_root
        ).astype(jnp.bfloat16)
        key_partial = (
            jnp.einsum("qk,qh->kh", grad_score, query_rows, preferred_element_type=jnp.float32)
            * inv_root
        ).astype(jnp.bfloat16)
        value_partial = jnp.einsum(
            "qk,qh->kh", prob_half, context_grad, preferred_element_type=jnp.float32
        ).astype(jnp.bfloat16)
        kv_partial = jnp.concatenate([key_partial, value_partial], axis=1).reshape(
            n_dep, tok_depth, 2 * head_dim
        )
        kv_grad = kv_partial[0].astype(jnp.float32)
        for s in range(1, n_dep):
            kv_grad = kv_grad + shift(kv_partial[s], DEP, n_dep, s).astype(jnp.float32)
        kv_grad = kv_grad.astype(jnp.bfloat16)
        grad_key, grad_value = kv_grad[:, :head_dim], kv_grad[:, head_dim:]

        grad_weight = None
        for depth in range(n_dep):
            piece = jnp.einsum(
                "zxcth,tf->zxchf",
                ctx_all[:, depth],
                rows_all[depth].reshape(tok_depth, feat),
                preferred_element_type=jnp.float32,
            )
            grad_weight = piece if grad_weight is None else grad_weight + piece
        grad_weight = grad_weight.reshape(n_zh * n_x * n_core * head_dim, feat)
        return (grad_weight, grad_query, grad_key, grad_value)

    return shards


def solution(mesh):
    n_row, n_col, n_dep = mesh.shape["row"], mesh.shape["col"], mesh.shape["dep"]
    n_zh, n_core = 2, 2
    n_x = n_col // (n_zh * n_core)
    fine = Mesh(
        mesh.devices.reshape(n_row, n_zh, n_x, n_core, n_dep), ("row",) + COL + (DEP,)
    )
    in_specs = (
        P("row", DEP, COL),
        P("row", COL),
        P(DEP, ("row",) + COL),
        P(DEP, ("row",) + COL),
        P(DEP, ("row",) + COL),
        P(),
    )
    out_specs = (
        P("row", COL),
        P(DEP, ("row",) + COL),
        P(DEP, ("row",) + COL),
        P(DEP, ("row",) + COL),
    )
    return jax.shard_map(
        make_shards(n_zh, n_x, n_core, n_row, n_dep),
        mesh=fine,
        in_specs=in_specs,
        out_specs=out_specs,
        check_vma=False,
    )
```

```python
import math

import jax
import jax.numpy as jnp
from jax import lax
from jax.sharding import Mesh
from jax.sharding import PartitionSpec as P

NEG_FILL = -1e30
COL = ("zh", "x", "core")
DEP = "zl"


def segment_count(positions, seg_ends):
    return jnp.sum((positions[:, None] >= seg_ends[None, :]).astype(jnp.int32), axis=1)


def shift(x, axis, n, s):
    return lax.ppermute(x, axis, [(i, (i + s) % n) for i in range(n)])


def shift_open(x, axis, n, s):
    return lax.ppermute(x, axis, [(i, i + s) for i in range(n) if 0 <= i + s < n])


def roll_rows(x, amount, axis):
    size = x.shape[axis]
    doubled = jnp.concatenate([x, x], axis=axis)
    return lax.dynamic_slice_in_dim(doubled, (size - amount) % size, size, axis=axis)


def rolled_gather(x, axis, n, stack_axis=0):
    parts = [x] + [shift(x, axis, n, -s) for s in range(1, n)]
    return jnp.stack(parts, axis=stack_axis)


def pp_reduce_scatter(x, axis, n, dim):
    me = lax.axis_index(axis)
    acc = lax.dynamic_index_in_dim(x, me, dim, keepdims=False).astype(jnp.float32)
    for s in range(1, n):
        send = lax.dynamic_index_in_dim(x, (me + s) % n, dim, keepdims=False)
        acc = acc + shift(send, axis, n, s).astype(jnp.float32)
    return acc


def make_shards(n_zh, n_x, n_core, n_row, n_dep):
    def shards(grad_out, out_weight, query_rows, key_rows, value_rows, seg_lengths):
        n_tok, feat = grad_out.shape[1], grad_out.shape[2]
        tok_depth = n_row * n_tok
        head_dim = query_rows.shape[1]
        inv_root = 1.0 / math.sqrt(head_dim)
        me_r = lax.axis_index("row")
        me_d = lax.axis_index(DEP)
        local = grad_out[0]
        grad_rows = rolled_gather(local, "row", n_row).reshape(tok_depth, feat)

        kv = jnp.concatenate([key_rows, value_rows], axis=1)
        packed = jnp.concatenate([kv, local.reshape(-1, 2 * head_dim)], axis=0)
        packed_all = rolled_gather(packed, DEP, n_dep)
        kv_all = packed_all[:, :tok_depth].reshape(n_dep * tok_depth, 2 * head_dim)
        keys_all, values_all = kv_all[:, :head_dim], kv_all[:, head_dim:]
        by_depth = roll_rows(packed_all[:, tok_depth:].reshape(n_dep, n_tok, feat), me_d, 0)

        src_depth = (me_d + jnp.arange(n_dep, dtype=jnp.int32)) % n_dep
        key_pos = (
            (src_depth * tok_depth)[:, None] + jnp.arange(tok_depth, dtype=jnp.int32)[None, :]
        ).reshape(-1)
        seg_ends = jnp.cumsum(seg_lengths)
        key_seg = segment_count(key_pos, seg_ends)
        query_pos = me_d * tok_depth + jnp.arange(tok_depth, dtype=jnp.int32)
        query_seg = segment_count(query_pos, seg_ends)
        allowed = (query_seg[:, None] == key_seg[None, :]) & (
            key_pos[None, :] <= query_pos[:, None]
        )
        scores = (
            jnp.einsum("qh,kh->qk", query_rows, keys_all, preferred_element_type=jnp.float32)
            * inv_root
        )
        masked = jnp.where(allowed, scores, NEG_FILL)
        row_max = jnp.max(masked, axis=1, keepdims=True)
        exponent = jnp.where(allowed, jnp.exp(masked - row_max), 0.0)
        row_sum = jnp.sum(exponent, axis=1, keepdims=True)
        prob_full = exponent / row_sum
        prob_half = prob_full.astype(jnp.bfloat16)
        context = jnp.dot(prob_half, values_all, preferred_element_type=jnp.float32).astype(
            jnp.bfloat16
        )

        rows_all = rolled_gather(by_depth, "row", n_row, stack_axis=1)
        context = roll_rows(context, -me_r * n_tok, 0)
        ctx_all = lax.all_gather(context[None], ("zh", DEP, "x", "core"), axis=0, tiled=True)
        ctx_all = ctx_all.reshape(n_zh, n_dep, n_x, n_core, tok_depth, head_dim)

        weight_perm = jnp.transpose(
            out_weight.reshape(n_zh, n_x, n_core, head_dim, feat), (2, 1, 0, 3, 4)
        ).reshape(-1, feat)
        partial = jnp.einsum(
            "tf,hf->th",
            grad_rows,
            weight_perm,
            preferred_element_type=jnp.float32,
        ).astype(jnp.bfloat16)
        partial = pp_reduce_scatter(
            partial.reshape(tok_depth, n_core, -1), "core", n_core, 1
        ).astype(jnp.bfloat16)
        partial = pp_reduce_scatter(partial.reshape(tok_depth, n_x, -1), "x", n_x, 1).astype(
            jnp.bfloat16
        )
        partial = pp_reduce_scatter(
            partial.reshape(tok_depth, n_zh, -1), "zh", n_zh, 1
        ).astype(jnp.bfloat16)
        context_grad = roll_rows(partial, me_r * n_tok, 0)

        grad_prob = jnp.dot(context_grad, values_all.T, preferred_element_type=jnp.float32)
        delta_row = jnp.sum(prob_full * grad_prob, axis=1, keepdims=True)
        grad_score = (prob_full * (grad_prob - delta_row)).astype(jnp.bfloat16)
        grad_query = (
            jnp.dot(grad_score, keys_all, preferred_element_type=jnp.float32) * inv_root
        ).astype(jnp.bfloat16)
        key_partial = (
            jnp.einsum("qk,qh->kh", grad_score, query_rows, preferred_element_type=jnp.float32)
            * inv_root
        ).astype(jnp.bfloat16)
        value_partial = jnp.einsum(
            "qk,qh->kh", prob_half, context_grad, preferred_element_type=jnp.float32
        ).astype(jnp.bfloat16)
        kv_partial = jnp.concatenate([key_partial, value_partial], axis=1).reshape(
            n_dep, tok_depth, 2 * head_dim
        )
        kv_grad = kv_partial[0].astype(jnp.float32)
        for s in range(1, n_dep):
            kv_grad = kv_grad + shift_open(kv_partial[s], DEP, n_dep, s - n_dep).astype(
                jnp.float32
            )
        kv_grad = kv_grad.astype(jnp.bfloat16)
        grad_key, grad_value = kv_grad[:, :head_dim], kv_grad[:, head_dim:]

        grad_weight = None
        for depth in range(n_dep):
            piece = jnp.einsum(
                "zxcth,tf->zxchf",
                ctx_all[:, depth],
                rows_all[depth].reshape(tok_depth, feat),
                preferred_element_type=jnp.float32,
            )
            grad_weight = piece if grad_weight is None else grad_weight + piece
        grad_weight = grad_weight.reshape(n_zh * n_x * n_core * head_dim, feat)
        return (grad_weight, grad_query, grad_key, grad_value)

    return shards


def solution(mesh):
    n_row, n_col, n_dep = mesh.shape["row"], mesh.shape["col"], mesh.shape["dep"]
    n_zh, n_core = 2, 2
    n_x = n_col // (n_zh * n_core)
    fine = Mesh(
        mesh.devices.reshape(n_row, n_zh, n_x, n_core, n_dep), ("row",) + COL + (DEP,)
    )
    in_specs = (
        P("row", DEP, COL),
        P("row", COL),
        P(DEP, ("row",) + COL),
        P(DEP, ("row",) + COL),
        P(DEP, ("row",) + COL),
        P(),
    )
    out_specs = (
        P("row", COL),
        P(DEP, ("row",) + COL),
        P(DEP, ("row",) + COL),
        P(DEP, ("row",) + COL),
    )
    return jax.shard_map(
        make_shards(n_zh, n_x, n_core, n_row, n_dep),
        mesh=fine,
        in_specs=in_specs,
        out_specs=out_specs,
        check_vma=False,
    )
```

```python
import math

import jax
import jax.numpy as jnp
from jax import lax
from jax.sharding import Mesh
from jax.sharding import PartitionSpec as P

NEG_FILL = -1e30
COL = ("zh", "x", "core")
DEP = "zl"


def segment_count(positions, seg_ends):
    return jnp.sum((positions[:, None] >= seg_ends[None, :]).astype(jnp.int32), axis=1)


def shift(x, axis, n, s):
    return lax.ppermute(x, axis, [(i, (i + s) % n) for i in range(n)])


def shift_open(x, axis, n, s):
    return lax.ppermute(x, axis, [(i, i + s) for i in range(n) if 0 <= i + s < n])


def roll_rows(x, amount, axis):
    size = x.shape[axis]
    doubled = jnp.concatenate([x, x], axis=axis)
    return lax.dynamic_slice_in_dim(doubled, (size - amount) % size, size, axis=axis)


def rolled_gather(x, axis, n, stack_axis=0):
    parts = [x] + [shift(x, axis, n, -s) for s in range(1, n)]
    return jnp.stack(parts, axis=stack_axis)


def pp_reduce_scatter(x, axis, n, dim):
    me = lax.axis_index(axis)
    acc = lax.dynamic_index_in_dim(x, me, dim, keepdims=False).astype(jnp.float32)
    for s in range(1, n):
        send = lax.dynamic_index_in_dim(x, (me + s) % n, dim, keepdims=False)
        acc = acc + shift(send, axis, n, s).astype(jnp.float32)
    return acc


def make_shards(n_zh, n_x, n_core, n_row, n_dep):
    def shards(grad_out, out_weight, query_rows, key_rows, value_rows, seg_lengths):
        n_tok, feat = grad_out.shape[1], grad_out.shape[2]
        tok_depth = n_row * n_tok
        head_dim = query_rows.shape[1]
        inv_root = 1.0 / math.sqrt(head_dim)
        me_r = lax.axis_index("row")
        me_d = lax.axis_index(DEP)
        local = grad_out[0]
        grad_rows = rolled_gather(local, "row", n_row).reshape(tok_depth, feat)

        kv = jnp.concatenate([key_rows, value_rows], axis=1)
        packed = jnp.concatenate([kv, local.reshape(-1, 2 * head_dim)], axis=0)
        packed_all = rolled_gather(packed, DEP, n_dep)
        kv_all = packed_all[:, :tok_depth].reshape(n_dep * tok_depth, 2 * head_dim)
        keys_all, values_all = kv_all[:, :head_dim], kv_all[:, head_dim:]
        by_depth = roll_rows(packed_all[:, tok_depth:].reshape(n_dep, n_tok, feat), me_d, 0)

        src_depth = (me_d + jnp.arange(n_dep, dtype=jnp.int32)) % n_dep
        key_pos = (
            (src_depth * tok_depth)[:, None] + jnp.arange(tok_depth, dtype=jnp.int32)[None, :]
        ).reshape(-1)
        seg_ends = jnp.cumsum(seg_lengths)
        key_seg = segment_count(key_pos, seg_ends)
        query_pos = me_d * tok_depth + jnp.arange(tok_depth, dtype=jnp.int32)
        query_seg = segment_count(query_pos, seg_ends)
        allowed = (query_seg[:, None] == key_seg[None, :]) & (
            key_pos[None, :] <= query_pos[:, None]
        )
        scores = (
            jnp.einsum("qh,kh->qk", query_rows, keys_all, preferred_element_type=jnp.float32)
            * inv_root
        )
        masked = jnp.where(allowed, scores, NEG_FILL)
        row_max = jnp.max(masked, axis=1, keepdims=True)
        exponent = jnp.where(allowed, jnp.exp(masked - row_max), 0.0)
        row_sum = jnp.sum(exponent, axis=1, keepdims=True)
        prob_full = exponent / row_sum
        prob_half = prob_full.astype(jnp.bfloat16)
        context = jnp.dot(prob_half, values_all, preferred_element_type=jnp.float32).astype(
            jnp.bfloat16
        )

        rows_all = rolled_gather(by_depth, "row", n_row, stack_axis=1)
        context = roll_rows(context, -me_r * n_tok, 0)

        weight_perm = jnp.transpose(
            out_weight.reshape(n_zh, n_x, n_core, head_dim, feat), (2, 1, 0, 3, 4)
        ).reshape(-1, feat)
        partial = jnp.einsum(
            "tf,hf->th", grad_rows, weight_perm, preferred_element_type=jnp.float32
        ).astype(jnp.bfloat16)
        partial = pp_reduce_scatter(
            partial.reshape(tok_depth, n_core, -1), "core", n_core, 1
        ).astype(jnp.bfloat16)
        context, partial = lax.optimization_barrier((context, partial))
        ctx_all = lax.all_gather(context[None], ("zh", DEP, "x", "core"), axis=0, tiled=True)
        ctx_all = ctx_all.reshape(n_zh, n_dep, n_x, n_core, tok_depth, head_dim)
        partial = pp_reduce_scatter(partial.reshape(tok_depth, n_x, -1), "x", n_x, 1).astype(
            jnp.bfloat16
        )
        partial = pp_reduce_scatter(
            partial.reshape(tok_depth, n_zh, -1), "zh", n_zh, 1
        ).astype(jnp.bfloat16)
        context_grad = roll_rows(partial, me_r * n_tok, 0)

        grad_prob = jnp.dot(context_grad, values_all.T, preferred_element_type=jnp.float32)
        delta_row = jnp.sum(prob_full * grad_prob, axis=1, keepdims=True)
        grad_score = (prob_full * (grad_prob - delta_row)).astype(jnp.bfloat16)
        grad_query = (
            jnp.dot(grad_score, keys_all, preferred_element_type=jnp.float32) * inv_root
        ).astype(jnp.bfloat16)
        key_partial = (
            jnp.einsum("qk,qh->kh", grad_score, query_rows, preferred_element_type=jnp.float32)
            * inv_root
        ).astype(jnp.bfloat16)
        value_partial = jnp.einsum(
            "qk,qh->kh", prob_half, context_grad, preferred_element_type=jnp.float32
        ).astype(jnp.bfloat16)
        kv_partial = jnp.concatenate([key_partial, value_partial], axis=1).reshape(
            n_dep, tok_depth, 2 * head_dim
        )
        kv_grad = kv_partial[0].astype(jnp.float32)
        for s in range(1, n_dep):
            kv_grad = kv_grad + shift_open(kv_partial[s], DEP, n_dep, s - n_dep).astype(
                jnp.float32
            )
        kv_grad = kv_grad.astype(jnp.bfloat16)
        grad_key, grad_value = kv_grad[:, :head_dim], kv_grad[:, head_dim:]

        grad_weight = None
        for depth in range(n_dep):
            piece = jnp.einsum(
                "zxcth,tf->zxchf",
                ctx_all[:, depth],
                rows_all[depth].reshape(tok_depth, feat),
                preferred_element_type=jnp.float32,
            )
            grad_weight = piece if grad_weight is None else grad_weight + piece
        grad_weight = grad_weight.reshape(n_zh * n_x * n_core * head_dim, feat)
        return (grad_weight, grad_query, grad_key, grad_value)

    return shards


def solution(mesh):
    n_row, n_col, n_dep = mesh.shape["row"], mesh.shape["col"], mesh.shape["dep"]
    n_zh, n_core = 2, 2
    n_x = n_col // (n_zh * n_core)
    fine = Mesh(
        mesh.devices.reshape(n_row, n_zh, n_x, n_core, n_dep), ("row",) + COL + (DEP,)
    )
    in_specs = (
        P("row", DEP, COL),
        P("row", COL),
        P(DEP, ("row",) + COL),
        P(DEP, ("row",) + COL),
        P(DEP, ("row",) + COL),
        P(),
    )
    out_specs = (
        P("row", COL),
        P(DEP, ("row",) + COL),
        P(DEP, ("row",) + COL),
        P(DEP, ("row",) + COL),
    )
    return jax.shard_map(
        make_shards(n_zh, n_x, n_core, n_row, n_dep),
        mesh=fine,
        in_specs=in_specs,
        out_specs=out_specs,
        check_vma=False,
    )
```

```python
import math

import jax
import jax.numpy as jnp
from jax import lax
from jax.sharding import Mesh
from jax.sharding import PartitionSpec as P

NEG_FILL = -1e30
COL = ("zh", "x", "core")
DEP = "zl"


def segment_count(positions, seg_ends):
    return jnp.sum((positions[:, None] >= seg_ends[None, :]).astype(jnp.int32), axis=1)


def shift(x, axis, n, s):
    return lax.ppermute(x, axis, [(i, (i + s) % n) for i in range(n)])


def shift_open(x, axis, n, s):
    return lax.ppermute(x, axis, [(i, i + s) for i in range(n) if 0 <= i + s < n])


def roll_rows(x, amount, axis):
    size = x.shape[axis]
    doubled = jnp.concatenate([x, x], axis=axis)
    return lax.dynamic_slice_in_dim(doubled, (size - amount) % size, size, axis=axis)


def rolled_gather(x, axis, n, stack_axis=0):
    parts = [x] + [shift(x, axis, n, -s) for s in range(1, n)]
    return jnp.stack(parts, axis=stack_axis)


def pp_reduce_scatter(x, axis, n, dim):
    me = lax.axis_index(axis)
    acc = lax.dynamic_index_in_dim(x, me, dim, keepdims=False).astype(jnp.float32)
    for s in range(1, n):
        send = lax.dynamic_index_in_dim(x, (me + s) % n, dim, keepdims=False)
        acc = acc + shift(send, axis, n, s).astype(jnp.float32)
    return acc


def make_shards(n_zh, n_x, n_core, n_row, n_dep):
    def shards(grad_out, out_weight, query_rows, key_rows, value_rows, seg_lengths):
        n_tok, feat = grad_out.shape[1], grad_out.shape[2]
        tok_depth = n_row * n_tok
        head_dim = query_rows.shape[1]
        inv_root = 1.0 / math.sqrt(head_dim)
        me_r = lax.axis_index("row")
        me_d = lax.axis_index(DEP)
        local = grad_out[0]
        grad_rows = rolled_gather(local, "row", n_row).reshape(tok_depth, feat)

        kv = jnp.concatenate([key_rows, value_rows], axis=1)
        packed = jnp.concatenate([kv, local.reshape(-1, 2 * head_dim)], axis=0)
        packed_all = rolled_gather(packed, DEP, n_dep)
        kv_all = packed_all[:, :tok_depth].reshape(n_dep * tok_depth, 2 * head_dim)
        keys_all, values_all = kv_all[:, :head_dim], kv_all[:, head_dim:]
        by_depth = roll_rows(packed_all[:, tok_depth:].reshape(n_dep, n_tok, feat), me_d, 0)

        src_depth = (me_d + jnp.arange(n_dep, dtype=jnp.int32)) % n_dep
        key_pos = (
            (src_depth * tok_depth)[:, None] + jnp.arange(tok_depth, dtype=jnp.int32)[None, :]
        ).reshape(-1)
        seg_ends = jnp.cumsum(seg_lengths)
        key_seg = segment_count(key_pos, seg_ends)
        query_pos = me_d * tok_depth + jnp.arange(tok_depth, dtype=jnp.int32)
        query_seg = segment_count(query_pos, seg_ends)
        allowed = (query_seg[:, None] == key_seg[None, :]) & (
            key_pos[None, :] <= query_pos[:, None]
        )
        scores = (
            jnp.einsum("qh,kh->qk", query_rows, keys_all, preferred_element_type=jnp.float32)
            * inv_root
        )
        masked = jnp.where(allowed, scores, NEG_FILL)
        row_max = jnp.max(masked, axis=1, keepdims=True)
        exponent = jnp.where(allowed, jnp.exp(masked - row_max), 0.0)
        row_sum = jnp.sum(exponent, axis=1, keepdims=True)
        prob_full = exponent / row_sum
        prob_half = prob_full.astype(jnp.bfloat16)
        context = jnp.dot(prob_half, values_all, preferred_element_type=jnp.float32).astype(
            jnp.bfloat16
        )

        rows_all = rolled_gather(by_depth, "row", n_row, stack_axis=1)
        context = roll_rows(context, -me_r * n_tok, 0)

        weight_perm = jnp.transpose(
            out_weight.reshape(n_zh, n_x, n_core, head_dim, feat), (2, 1, 0, 3, 4)
        ).reshape(-1, feat)
        partial = jnp.einsum(
            "tf,hf->th", grad_rows, weight_perm, preferred_element_type=jnp.float32
        ).astype(jnp.bfloat16)
        partial = pp_reduce_scatter(
            partial.reshape(tok_depth, n_core, -1), "core", n_core, 1
        ).astype(jnp.bfloat16)
        context, partial = lax.optimization_barrier((context, partial))
        ctx_own = lax.all_gather(context[None], ("zh", DEP, "x"), axis=0, tiled=True)
        ctx_own = ctx_own.reshape(n_zh, n_dep, n_x, tok_depth, head_dim)
        ctx_other = shift(ctx_own, "core", n_core, 1)
        partial = pp_reduce_scatter(partial.reshape(tok_depth, n_x, -1), "x", n_x, 1).astype(
            jnp.bfloat16
        )
        partial = pp_reduce_scatter(
            partial.reshape(tok_depth, n_zh, -1), "zh", n_zh, 1
        ).astype(jnp.bfloat16)
        context_grad = roll_rows(partial, me_r * n_tok, 0)

        grad_prob = jnp.dot(context_grad, values_all.T, preferred_element_type=jnp.float32)
        delta_row = jnp.sum(prob_full * grad_prob, axis=1, keepdims=True)
        grad_score = (prob_full * (grad_prob - delta_row)).astype(jnp.bfloat16)
        grad_query = (
            jnp.dot(grad_score, keys_all, preferred_element_type=jnp.float32) * inv_root
        ).astype(jnp.bfloat16)
        key_partial = (
            jnp.einsum("qk,qh->kh", grad_score, query_rows, preferred_element_type=jnp.float32)
            * inv_root
        ).astype(jnp.bfloat16)
        value_partial = jnp.einsum(
            "qk,qh->kh", prob_half, context_grad, preferred_element_type=jnp.float32
        ).astype(jnp.bfloat16)
        kv_partial = jnp.concatenate([key_partial, value_partial], axis=1).reshape(
            n_dep, tok_depth, 2 * head_dim
        )
        kv_grad = kv_partial[0].astype(jnp.float32)
        for s in range(1, n_dep):
            kv_grad = kv_grad + shift_open(kv_partial[s], DEP, n_dep, s - n_dep).astype(
                jnp.float32
            )
        kv_grad = kv_grad.astype(jnp.bfloat16)
        grad_key, grad_value = kv_grad[:, :head_dim], kv_grad[:, head_dim:]

        first_core = lax.axis_index("core") == 0
        grad_weight = None
        for depth in range(n_dep):
            own, other = ctx_own[:, depth], ctx_other[:, depth]
            ctx_depth = jnp.stack(
                [jnp.where(first_core, own, other), jnp.where(first_core, other, own)], axis=2
            )
            piece = jnp.einsum(
                "zxcth,tf->zxchf",
                ctx_depth,
                rows_all[depth].reshape(tok_depth, feat),
                preferred_element_type=jnp.float32,
            )
            grad_weight = piece if grad_weight is None else grad_weight + piece
        grad_weight = grad_weight.reshape(n_zh * n_x * n_core * head_dim, feat)
        return (grad_weight, grad_query, grad_key, grad_value)

    return shards


def solution(mesh):
    n_row, n_col, n_dep = mesh.shape["row"], mesh.shape["col"], mesh.shape["dep"]
    n_zh, n_core = 2, 2
    n_x = n_col // (n_zh * n_core)
    fine = Mesh(
        mesh.devices.reshape(n_row, n_zh, n_x, n_core, n_dep), ("row",) + COL + (DEP,)
    )
    in_specs = (
        P("row", DEP, COL),
        P("row", COL),
        P(DEP, ("row",) + COL),
        P(DEP, ("row",) + COL),
        P(DEP, ("row",) + COL),
        P(),
    )
    out_specs = (
        P("row", COL),
        P(DEP, ("row",) + COL),
        P(DEP, ("row",) + COL),
        P(DEP, ("row",) + COL),
    )
    return jax.shard_map(
        make_shards(n_zh, n_x, n_core, n_row, n_dep),
        mesh=fine,
        in_specs=in_specs,
        out_specs=out_specs,
        check_vma=False,
    )
```

```python
import math

import jax
import jax.numpy as jnp
from jax import lax
from jax.sharding import Mesh
from jax.sharding import PartitionSpec as P

NEG_FILL = -1e30
COL = ("zh", "x", "core")
DEP = "zl"


def segment_count(positions, seg_ends):
    return jnp.sum((positions[:, None] >= seg_ends[None, :]).astype(jnp.int32), axis=1)


def shift(x, axis, n, s):
    return lax.ppermute(x, axis, [(i, (i + s) % n) for i in range(n)])


def shift_open(x, axis, n, s):
    return lax.ppermute(x, axis, [(i, i + s) for i in range(n) if 0 <= i + s < n])


def roll_rows(x, amount, axis):
    size = x.shape[axis]
    doubled = jnp.concatenate([x, x], axis=axis)
    return lax.dynamic_slice_in_dim(doubled, (size - amount) % size, size, axis=axis)


def rolled_gather(x, axis, n, stack_axis=0):
    parts = [x] + [shift(x, axis, n, -s) for s in range(1, n)]
    return jnp.stack(parts, axis=stack_axis)


def pp_reduce_scatter(x, axis, n, dim):
    me = lax.axis_index(axis)
    acc = lax.dynamic_index_in_dim(x, me, dim, keepdims=False).astype(jnp.float32)
    for s in range(1, n):
        send = lax.dynamic_index_in_dim(x, (me + s) % n, dim, keepdims=False)
        acc = acc + shift(send, axis, n, s).astype(jnp.float32)
    return acc


def make_shards(n_zh, n_x, n_core, n_row, n_dep):
    def shards(grad_out, out_weight, query_rows, key_rows, value_rows, seg_lengths):
        n_tok, feat = grad_out.shape[1], grad_out.shape[2]
        tok_depth = n_row * n_tok
        head_dim = query_rows.shape[1]
        inv_root = 1.0 / math.sqrt(head_dim)
        me_r = lax.axis_index("row")
        me_d = lax.axis_index(DEP)
        local = grad_out[0]
        grad_rows = rolled_gather(local, "row", n_row).reshape(tok_depth, feat)

        kv = jnp.concatenate([key_rows, value_rows], axis=1)
        packed = jnp.concatenate([kv, local.reshape(-1, 2 * head_dim)], axis=0)
        packed_all = rolled_gather(packed, DEP, n_dep)
        kv_all = packed_all[:, :tok_depth].reshape(n_dep * tok_depth, 2 * head_dim)
        keys_all, values_all = kv_all[:, :head_dim], kv_all[:, head_dim:]
        by_depth = roll_rows(packed_all[:, tok_depth:].reshape(n_dep, n_tok, feat), me_d, 0)

        src_depth = (me_d + jnp.arange(n_dep, dtype=jnp.int32)) % n_dep
        key_pos = (
            (src_depth * tok_depth)[:, None] + jnp.arange(tok_depth, dtype=jnp.int32)[None, :]
        ).reshape(-1)
        seg_ends = jnp.cumsum(seg_lengths)
        key_seg = segment_count(key_pos, seg_ends)
        query_pos = me_d * tok_depth + jnp.arange(tok_depth, dtype=jnp.int32)
        query_seg = segment_count(query_pos, seg_ends)
        allowed = (query_seg[:, None] == key_seg[None, :]) & (
            key_pos[None, :] <= query_pos[:, None]
        )
        scores = (
            jnp.einsum("qh,kh->qk", query_rows, keys_all, preferred_element_type=jnp.float32)
            * inv_root
        )
        masked = jnp.where(allowed, scores, NEG_FILL)
        row_max = jnp.max(masked, axis=1, keepdims=True)
        exponent = jnp.where(allowed, jnp.exp(masked - row_max), 0.0)
        row_sum = jnp.sum(exponent, axis=1, keepdims=True)
        prob_full = exponent / row_sum
        prob_half = prob_full.astype(jnp.bfloat16)
        context = jnp.dot(prob_half, values_all, preferred_element_type=jnp.float32).astype(
            jnp.bfloat16
        )

        rows_all = rolled_gather(by_depth, "row", n_row, stack_axis=1)
        context = roll_rows(context, -me_r * n_tok, 0)

        weight_perm = jnp.transpose(
            out_weight.reshape(n_zh, n_x, n_core, head_dim, feat), (2, 1, 0, 3, 4)
        ).reshape(-1, feat)
        partial = jnp.einsum(
            "tf,hf->th", grad_rows, weight_perm, preferred_element_type=jnp.float32
        ).astype(jnp.bfloat16)
        partial = pp_reduce_scatter(
            partial.reshape(tok_depth, n_core, -1), "core", n_core, 1
        ).astype(jnp.bfloat16)
        context, partial = lax.optimization_barrier((context, partial))
        ctx_own = lax.all_gather(context[None], ("zh", DEP, "x"), axis=0, tiled=True)
        ctx_own = ctx_own.reshape(n_zh, n_dep, n_x, tok_depth, head_dim)
        partial = pp_reduce_scatter(partial.reshape(tok_depth, n_x, -1), "x", n_x, 1).astype(
            jnp.bfloat16
        )
        partial = pp_reduce_scatter(
            partial.reshape(tok_depth, n_zh, -1), "zh", n_zh, 1
        ).astype(jnp.bfloat16)
        context_grad = roll_rows(partial, me_r * n_tok, 0)

        grad_prob = jnp.dot(context_grad, values_all.T, preferred_element_type=jnp.float32)
        delta_row = jnp.sum(prob_full * grad_prob, axis=1, keepdims=True)
        grad_score = (prob_full * (grad_prob - delta_row)).astype(jnp.bfloat16)
        grad_query = (
            jnp.dot(grad_score, keys_all, preferred_element_type=jnp.float32) * inv_root
        ).astype(jnp.bfloat16)
        key_partial = (
            jnp.einsum("qk,qh->kh", grad_score, query_rows, preferred_element_type=jnp.float32)
            * inv_root
        ).astype(jnp.bfloat16)
        value_partial = jnp.einsum(
            "qk,qh->kh", prob_half, context_grad, preferred_element_type=jnp.float32
        ).astype(jnp.bfloat16)
        kv_partial = jnp.concatenate([key_partial, value_partial], axis=1).reshape(
            n_dep, tok_depth, 2 * head_dim
        )
        kv_grad = kv_partial[0].astype(jnp.float32)
        for s in range(1, n_dep):
            kv_grad = kv_grad + shift_open(kv_partial[s], DEP, n_dep, s - n_dep).astype(
                jnp.float32
            )
        kv_grad = kv_grad.astype(jnp.bfloat16)
        grad_key, grad_value = kv_grad[:, :head_dim], kv_grad[:, head_dim:]
        ctx_own, kv_grad, rows_all = lax.optimization_barrier((ctx_own, kv_grad, rows_all))
        ctx_other = shift(ctx_own, "core", n_core, 1)

        first_core = lax.axis_index("core") == 0
        grad_weight = None
        for depth in range(n_dep):
            own, other = ctx_own[:, depth], ctx_other[:, depth]
            ctx_depth = jnp.stack(
                [jnp.where(first_core, own, other), jnp.where(first_core, other, own)], axis=2
            )
            piece = jnp.einsum(
                "zxcth,tf->zxchf",
                ctx_depth,
                rows_all[depth].reshape(tok_depth, feat),
                preferred_element_type=jnp.float32,
            )
            grad_weight = piece if grad_weight is None else grad_weight + piece
        grad_weight = grad_weight.reshape(n_zh * n_x * n_core * head_dim, feat)
        return (grad_weight, grad_query, grad_key, grad_value)

    return shards


def solution(mesh):
    n_row, n_col, n_dep = mesh.shape["row"], mesh.shape["col"], mesh.shape["dep"]
    n_zh, n_core = 2, 2
    n_x = n_col // (n_zh * n_core)
    fine = Mesh(
        mesh.devices.reshape(n_row, n_zh, n_x, n_core, n_dep), ("row",) + COL + (DEP,)
    )
    in_specs = (
        P("row", DEP, COL),
        P("row", COL),
        P(DEP, ("row",) + COL),
        P(DEP, ("row",) + COL),
        P(DEP, ("row",) + COL),
        P(),
    )
    out_specs = (
        P("row", COL),
        P(DEP, ("row",) + COL),
        P(DEP, ("row",) + COL),
        P(DEP, ("row",) + COL),
    )
    return jax.shard_map(
        make_shards(n_zh, n_x, n_core, n_row, n_dep),
        mesh=fine,
        in_specs=in_specs,
        out_specs=out_specs,
        check_vma=False,
    )
```

```python
import math

import jax
import jax.numpy as jnp
from jax import lax
from jax.sharding import Mesh
from jax.sharding import PartitionSpec as P

NEG_FILL = -1e30
COL = ("zh", "x", "core")
DEP = "zl"


def segment_count(positions, seg_ends):
    return jnp.sum((positions[:, None] >= seg_ends[None, :]).astype(jnp.int32), axis=1)


def shift(x, axis, n, s):
    return lax.ppermute(x, axis, [(i, (i + s) % n) for i in range(n)])


def shift_open(x, axis, n, s):
    return lax.ppermute(x, axis, [(i, i + s) for i in range(n) if 0 <= i + s < n])


def roll_rows(x, amount, axis):
    size = x.shape[axis]
    doubled = jnp.concatenate([x, x], axis=axis)
    return lax.dynamic_slice_in_dim(doubled, (size - amount) % size, size, axis=axis)


def rolled_gather(x, axis, n, stack_axis=0):
    parts = [x] + [shift(x, axis, n, -s) for s in range(1, n)]
    return jnp.stack(parts, axis=stack_axis)


def pp_reduce_scatter(x, axis, n, dim):
    me = lax.axis_index(axis)
    acc = lax.dynamic_index_in_dim(x, me, dim, keepdims=False).astype(jnp.float32)
    for s in range(1, n):
        send = lax.dynamic_index_in_dim(x, (me + s) % n, dim, keepdims=False)
        acc = acc + shift(send, axis, n, s).astype(jnp.float32)
    return acc


def make_shards(n_zh, n_x, n_core, n_row, n_dep):
    def shards(grad_out, out_weight, query_rows, key_rows, value_rows, seg_lengths):
        n_tok, feat = grad_out.shape[1], grad_out.shape[2]
        tok_depth = n_row * n_tok
        head_dim = query_rows.shape[1]
        inv_root = 1.0 / math.sqrt(head_dim)
        me_r = lax.axis_index("row")
        me_d = lax.axis_index(DEP)
        local = grad_out[0]
        grad_rows = rolled_gather(local, "row", n_row).reshape(tok_depth, feat)

        kv = jnp.concatenate([key_rows, value_rows], axis=1)
        packed = jnp.concatenate([kv, local.reshape(-1, 2 * head_dim)], axis=0)
        packed_all = rolled_gather(packed, DEP, n_dep)
        kv_all = packed_all[:, :tok_depth].reshape(n_dep * tok_depth, 2 * head_dim)
        keys_all, values_all = kv_all[:, :head_dim], kv_all[:, head_dim:]
        by_depth = roll_rows(packed_all[:, tok_depth:].reshape(n_dep, n_tok, feat), me_d, 0)

        src_depth = (me_d + jnp.arange(n_dep, dtype=jnp.int32)) % n_dep
        key_pos = (
            (src_depth * tok_depth)[:, None] + jnp.arange(tok_depth, dtype=jnp.int32)[None, :]
        ).reshape(-1)
        seg_ends = jnp.cumsum(seg_lengths)
        key_seg = segment_count(key_pos, seg_ends)
        query_pos = me_d * tok_depth + jnp.arange(tok_depth, dtype=jnp.int32)
        query_seg = segment_count(query_pos, seg_ends)
        allowed = (query_seg[:, None] == key_seg[None, :]) & (
            key_pos[None, :] <= query_pos[:, None]
        )
        scores = (
            jnp.einsum("qh,kh->qk", query_rows, keys_all, preferred_element_type=jnp.float32)
            * inv_root
        )
        masked = jnp.where(allowed, scores, NEG_FILL)
        row_max = jnp.max(masked, axis=1, keepdims=True)
        exponent = jnp.where(allowed, jnp.exp(masked - row_max), 0.0)
        row_sum = jnp.sum(exponent, axis=1, keepdims=True)
        prob_full = exponent / row_sum
        prob_half = prob_full.astype(jnp.bfloat16)
        context = jnp.dot(prob_half, values_all, preferred_element_type=jnp.float32).astype(
            jnp.bfloat16
        )

        rows_all = rolled_gather(by_depth, "row", n_row, stack_axis=1)
        context = roll_rows(context, -me_r * n_tok, 0)

        weight_perm = jnp.transpose(
            out_weight.reshape(n_zh, n_x, n_core, head_dim, feat), (2, 1, 0, 3, 4)
        ).reshape(-1, feat)
        partial = jnp.einsum(
            "tf,hf->th", grad_rows, weight_perm, preferred_element_type=jnp.float32
        ).astype(jnp.bfloat16)
        partial = pp_reduce_scatter(
            partial.reshape(tok_depth, n_core, -1), "core", n_core, 1
        ).astype(jnp.bfloat16)
        context, partial = lax.optimization_barrier((context, partial))
        ctx_own = lax.all_gather(context[None], ("zh", DEP, "x"), axis=0, tiled=True)
        ctx_own = ctx_own.reshape(n_zh, n_dep, n_x, tok_depth, head_dim)
        partial = pp_reduce_scatter(partial.reshape(tok_depth, n_x, -1), "x", n_x, 1).astype(
            jnp.bfloat16
        )
        partial = pp_reduce_scatter(
            partial.reshape(tok_depth, n_zh, -1), "zh", n_zh, 1
        ).astype(jnp.bfloat16)
        context_grad = roll_rows(partial, me_r * n_tok, 0)

        grad_prob = jnp.dot(context_grad, values_all.T, preferred_element_type=jnp.float32)
        delta_row = jnp.sum(prob_full * grad_prob, axis=1, keepdims=True)
        grad_score = (prob_full * (grad_prob - delta_row)).astype(jnp.bfloat16)
        grad_query = (
            jnp.dot(grad_score, keys_all, preferred_element_type=jnp.float32) * inv_root
        ).astype(jnp.bfloat16)
        key_partial = (
            jnp.einsum("qk,qh->kh", grad_score, query_rows, preferred_element_type=jnp.float32)
            * inv_root
        ).astype(jnp.bfloat16)
        value_partial = jnp.einsum(
            "qk,qh->kh", prob_half, context_grad, preferred_element_type=jnp.float32
        ).astype(jnp.bfloat16)
        kv_partial = jnp.concatenate([key_partial, value_partial], axis=1).reshape(
            n_dep, tok_depth, 2 * head_dim
        )
        kv_grad = kv_partial[0].astype(jnp.float32)
        for s in range(1, n_dep):
            kv_grad = kv_grad + shift_open(kv_partial[s], DEP, n_dep, s - n_dep).astype(
                jnp.float32
            )
        kv_grad = kv_grad.astype(jnp.bfloat16)
        grad_key, grad_value = kv_grad[:, :head_dim], kv_grad[:, head_dim:]
        ctx_own, kv_grad, rows_all = lax.optimization_barrier((ctx_own, kv_grad, rows_all))
        ctx_other = shift(ctx_own, "core", n_core, 1)

        def half(ctx_half):
            total = None
            for depth in range(n_dep):
                piece = jnp.einsum(
                    "zxth,tf->zxhf",
                    ctx_half[:, depth],
                    rows_all[depth].reshape(tok_depth, feat),
                    preferred_element_type=jnp.float32,
                )
                total = piece if total is None else total + piece
            return total[:, :, None]

        me_core = lax.axis_index("core")
        grad_weight = jnp.zeros((n_zh, n_x, n_core, head_dim, feat), jnp.float32)
        grad_weight = lax.dynamic_update_slice_in_dim(grad_weight, half(ctx_own), me_core, 2)
        grad_weight = lax.dynamic_update_slice_in_dim(
            grad_weight, half(ctx_other), n_core - 1 - me_core, 2
        )
        grad_weight = grad_weight.reshape(n_zh * n_x * n_core * head_dim, feat)
        return (grad_weight, grad_query, grad_key, grad_value)

    return shards


def solution(mesh):
    n_row, n_col, n_dep = mesh.shape["row"], mesh.shape["col"], mesh.shape["dep"]
    n_zh, n_core = 2, 2
    n_x = n_col // (n_zh * n_core)
    fine = Mesh(
        mesh.devices.reshape(n_row, n_zh, n_x, n_core, n_dep), ("row",) + COL + (DEP,)
    )
    in_specs = (
        P("row", DEP, COL),
        P("row", COL),
        P(DEP, ("row",) + COL),
        P(DEP, ("row",) + COL),
        P(DEP, ("row",) + COL),
        P(),
    )
    out_specs = (
        P("row", COL),
        P(DEP, ("row",) + COL),
        P(DEP, ("row",) + COL),
        P(DEP, ("row",) + COL),
    )
    return jax.shard_map(
        make_shards(n_zh, n_x, n_core, n_row, n_dep),
        mesh=fine,
        in_specs=in_specs,
        out_specs=out_specs,
        check_vma=False,
    )
```

```python
import math

import jax
import jax.numpy as jnp
from jax import lax
from jax.sharding import Mesh
from jax.sharding import PartitionSpec as P

NEG_FILL = -1e30
COL = ("zh", "x", "core")
DEP = "zl"


def segment_count(positions, seg_ends):
    return jnp.sum((positions[:, None] >= seg_ends[None, :]).astype(jnp.int32), axis=1)


def shift(x, axis, n, s):
    return lax.ppermute(x, axis, [(i, (i + s) % n) for i in range(n)])


def shift_open(x, axis, n, s):
    return lax.ppermute(x, axis, [(i, i + s) for i in range(n) if 0 <= i + s < n])


def roll_rows(x, amount, axis):
    size = x.shape[axis]
    doubled = jnp.concatenate([x, x], axis=axis)
    return lax.dynamic_slice_in_dim(doubled, (size - amount) % size, size, axis=axis)


def rolled_gather(x, axis, n, stack_axis=0):
    parts = [x] + [shift(x, axis, n, -s) for s in range(1, n)]
    return jnp.stack(parts, axis=stack_axis)


def pp_reduce_scatter(x, axis, n, dim):
    me = lax.axis_index(axis)
    acc = lax.dynamic_index_in_dim(x, me, dim, keepdims=False).astype(jnp.float32)
    for s in range(1, n):
        send = lax.dynamic_index_in_dim(x, (me + s) % n, dim, keepdims=False)
        acc = acc + shift(send, axis, n, s).astype(jnp.float32)
    return acc


def pp_reduce_scatter_cols(x, axis, n):
    me = lax.axis_index(axis)
    width = x.shape[1] // n
    acc = lax.dynamic_slice_in_dim(x, me * width, width, axis=1).astype(jnp.float32)
    for s in range(1, n):
        send = lax.dynamic_slice_in_dim(x, ((me + s) % n) * width, width, axis=1)
        acc = acc + shift(send, axis, n, s).astype(jnp.float32)
    return acc


def make_shards(n_zh, n_x, n_core, n_row, n_dep):
    def shards(grad_out, out_weight, query_rows, key_rows, value_rows, seg_lengths):
        n_tok, feat = grad_out.shape[1], grad_out.shape[2]
        tok_depth = n_row * n_tok
        head_dim = query_rows.shape[1]
        inv_root = 1.0 / math.sqrt(head_dim)
        me_r = lax.axis_index("row")
        me_d = lax.axis_index(DEP)
        local = grad_out[0]
        grad_rows = rolled_gather(local, "row", n_row).reshape(tok_depth, feat)

        kv = jnp.concatenate([key_rows, value_rows], axis=1)
        packed = jnp.concatenate([kv, local.reshape(-1, 2 * head_dim)], axis=0)
        packed_all = rolled_gather(packed, DEP, n_dep)
        kv_all = packed_all[:, :tok_depth].reshape(n_dep * tok_depth, 2 * head_dim)
        keys_all, values_all = kv_all[:, :head_dim], kv_all[:, head_dim:]
        by_depth = roll_rows(packed_all[:, tok_depth:].reshape(n_dep, n_tok, feat), me_d, 0)

        src_depth = (me_d + jnp.arange(n_dep, dtype=jnp.int32)) % n_dep
        key_pos = (
            (src_depth * tok_depth)[:, None] + jnp.arange(tok_depth, dtype=jnp.int32)[None, :]
        ).reshape(-1)
        seg_ends = jnp.cumsum(seg_lengths)
        key_seg = segment_count(key_pos, seg_ends)
        query_pos = me_d * tok_depth + jnp.arange(tok_depth, dtype=jnp.int32)
        query_seg = segment_count(query_pos, seg_ends)
        allowed = (query_seg[:, None] == key_seg[None, :]) & (
            key_pos[None, :] <= query_pos[:, None]
        )
        scores = (
            jnp.einsum("qh,kh->qk", query_rows, keys_all, preferred_element_type=jnp.float32)
            * inv_root
        )
        masked = jnp.where(allowed, scores, NEG_FILL)
        row_max = jnp.max(masked, axis=1, keepdims=True)
        exponent = jnp.where(allowed, jnp.exp(masked - row_max), 0.0)
        row_sum = jnp.sum(exponent, axis=1, keepdims=True)
        prob_full = exponent / row_sum
        prob_half = prob_full.astype(jnp.bfloat16)
        context = jnp.dot(prob_half, values_all, preferred_element_type=jnp.float32).astype(
            jnp.bfloat16
        )

        rows_all = rolled_gather(by_depth, "row", n_row, stack_axis=1)
        context = roll_rows(context, -me_r * n_tok, 0)

        weight_perm = jnp.transpose(
            out_weight.reshape(n_zh, n_x, n_core, head_dim, feat), (2, 1, 0, 3, 4)
        ).reshape(-1, feat)
        partial = jnp.einsum(
            "tf,hf->th", grad_rows, weight_perm, preferred_element_type=jnp.float32
        ).astype(jnp.bfloat16)
        partial = pp_reduce_scatter_cols(partial, "core", n_core).astype(jnp.bfloat16)
        context, partial = lax.optimization_barrier((context, partial))
        ctx_all = lax.all_gather(context[None], ("zh", DEP, "x", "core"), axis=0, tiled=True)
        ctx_all = ctx_all.reshape(n_zh, n_dep, n_x, n_core, tok_depth, head_dim)
        partial = pp_reduce_scatter_cols(partial, "x", n_x).astype(jnp.bfloat16)
        partial = pp_reduce_scatter_cols(partial, "zh", n_zh).astype(jnp.bfloat16)
        context_grad = roll_rows(partial, me_r * n_tok, 0)

        grad_prob = jnp.dot(context_grad, values_all.T, preferred_element_type=jnp.float32)
        delta_row = jnp.sum(prob_full * grad_prob, axis=1, keepdims=True)
        grad_score = (prob_full * (grad_prob - delta_row)).astype(jnp.bfloat16)
        grad_query = (
            jnp.dot(grad_score, keys_all, preferred_element_type=jnp.float32) * inv_root
        ).astype(jnp.bfloat16)
        key_partial = (
            jnp.einsum("qk,qh->kh", grad_score, query_rows, preferred_element_type=jnp.float32)
            * inv_root
        ).astype(jnp.bfloat16)
        value_partial = jnp.einsum(
            "qk,qh->kh", prob_half, context_grad, preferred_element_type=jnp.float32
        ).astype(jnp.bfloat16)
        kv_partial = jnp.concatenate([key_partial, value_partial], axis=1).reshape(
            n_dep, tok_depth, 2 * head_dim
        )
        kv_grad = kv_partial[0].astype(jnp.float32)
        for s in range(1, n_dep):
            kv_grad = kv_grad + shift_open(kv_partial[s], DEP, n_dep, s - n_dep).astype(
                jnp.float32
            )
        kv_grad = kv_grad.astype(jnp.bfloat16)
        grad_key, grad_value = kv_grad[:, :head_dim], kv_grad[:, head_dim:]

        grad_weight = None
        for depth in range(n_dep):
            piece = jnp.einsum(
                "zxcth,tf->zxchf",
                ctx_all[:, depth],
                rows_all[depth].reshape(tok_depth, feat),
                preferred_element_type=jnp.float32,
            )
            grad_weight = piece if grad_weight is None else grad_weight + piece
            if depth < n_dep - 1:
                grad_weight = lax.optimization_barrier(grad_weight)
        grad_weight = grad_weight.reshape(n_zh * n_x * n_core * head_dim, feat)
        return (grad_weight, grad_query, grad_key, grad_value)

    return shards


def solution(mesh):
    n_row, n_col, n_dep = mesh.shape["row"], mesh.shape["col"], mesh.shape["dep"]
    n_zh, n_core = 2, 2
    n_x = n_col // (n_zh * n_core)
    fine = Mesh(
        mesh.devices.reshape(n_row, n_zh, n_x, n_core, n_dep), ("row",) + COL + (DEP,)
    )
    in_specs = (
        P("row", DEP, COL),
        P("row", COL),
        P(DEP, ("row",) + COL),
        P(DEP, ("row",) + COL),
        P(DEP, ("row",) + COL),
        P(),
    )
    out_specs = (
        P("row", COL),
        P(DEP, ("row",) + COL),
        P(DEP, ("row",) + COL),
        P(DEP, ("row",) + COL),
    )
    return jax.shard_map(
        make_shards(n_zh, n_x, n_core, n_row, n_dep),
        mesh=fine,
        in_specs=in_specs,
        out_specs=out_specs,
        check_vma=False,
    )
```

```python
import math

import jax
import jax.numpy as jnp
from jax import lax
from jax.sharding import Mesh
from jax.sharding import PartitionSpec as P

NEG_FILL = -1e30
FAR = 1 << 30
COL = ("zh", "x", "core")
DEP = "zl"


def segment_count(positions, seg_ends):
    return jnp.sum((positions[:, None] >= seg_ends[None, :]).astype(jnp.int32), axis=1)


def shift(x, axis, n, s):
    return lax.ppermute(x, axis, [(i, (i + s) % n) for i in range(n)])


def shift_open(x, axis, n, s):
    return lax.ppermute(x, axis, [(i, i + s) for i in range(n) if 0 <= i + s < n])


def roll_rows(x, amount, axis):
    size = x.shape[axis]
    doubled = jnp.concatenate([x, x], axis=axis)
    return lax.dynamic_slice_in_dim(doubled, (size - amount) % size, size, axis=axis)


def rolled_gather(x, axis, n, stack_axis=0):
    parts = [x] + [shift(x, axis, n, -s) for s in range(1, n)]
    return jnp.stack(parts, axis=stack_axis)


def pp_reduce_scatter(x, axis, n, dim):
    me = lax.axis_index(axis)
    acc = lax.dynamic_index_in_dim(x, me, dim, keepdims=False).astype(jnp.float32)
    for s in range(1, n):
        send = lax.dynamic_index_in_dim(x, (me + s) % n, dim, keepdims=False)
        acc = acc + shift(send, axis, n, s).astype(jnp.float32)
    return acc


def pp_reduce_scatter_cols(x, axis, n):
    me = lax.axis_index(axis)
    width = x.shape[1] // n
    acc = lax.dynamic_slice_in_dim(x, me * width, width, axis=1).astype(jnp.float32)
    for s in range(1, n):
        send = lax.dynamic_slice_in_dim(x, ((me + s) % n) * width, width, axis=1)
        acc = acc + shift(send, axis, n, s).astype(jnp.float32)
    return acc


def make_shards(n_zh, n_x, n_core, n_row, n_dep):
    def shards(grad_out, out_weight, query_rows, key_rows, value_rows, seg_lengths):
        n_tok, feat = grad_out.shape[1], grad_out.shape[2]
        tok_depth = n_row * n_tok
        head_dim = query_rows.shape[1]
        inv_root = 1.0 / math.sqrt(head_dim)
        me_r = lax.axis_index("row")
        me_d = lax.axis_index(DEP)
        local = grad_out[0]
        grad_rows = rolled_gather(local, "row", n_row).reshape(tok_depth, feat)

        kv = jnp.concatenate([key_rows, value_rows], axis=1)
        kv_all = jnp.stack(
            [kv] + [shift_open(kv, DEP, n_dep, t) for t in range(1, n_dep)], axis=0
        ).reshape(n_dep * tok_depth, 2 * head_dim)
        keys_all, values_all = kv_all[:, :head_dim], kv_all[:, head_dim:]
        by_depth = roll_rows(rolled_gather(local, DEP, n_dep), me_d, 0)

        src_depth = me_d - jnp.arange(n_dep, dtype=jnp.int32)
        key_pos = (
            jnp.where(src_depth >= 0, src_depth * tok_depth, FAR)[:, None]
            + jnp.arange(tok_depth, dtype=jnp.int32)[None, :]
        ).reshape(-1)
        seg_ends = jnp.cumsum(seg_lengths)
        key_seg = segment_count(key_pos, seg_ends)
        query_pos = me_d * tok_depth + jnp.arange(tok_depth, dtype=jnp.int32)
        query_seg = segment_count(query_pos, seg_ends)
        allowed = (query_seg[:, None] == key_seg[None, :]) & (
            key_pos[None, :] <= query_pos[:, None]
        )
        scores = (
            jnp.einsum("qh,kh->qk", query_rows, keys_all, preferred_element_type=jnp.float32)
            * inv_root
        )
        masked = jnp.where(allowed, scores, NEG_FILL)
        row_max = jnp.max(masked, axis=1, keepdims=True)
        exponent = jnp.where(allowed, jnp.exp(masked - row_max), 0.0)
        row_sum = jnp.sum(exponent, axis=1, keepdims=True)
        prob_full = exponent / row_sum
        prob_half = prob_full.astype(jnp.bfloat16)
        context = jnp.dot(prob_half, values_all, preferred_element_type=jnp.float32).astype(
            jnp.bfloat16
        )

        rows_all = rolled_gather(by_depth, "row", n_row, stack_axis=1)
        context = roll_rows(context, -me_r * n_tok, 0)

        weight_perm = jnp.transpose(
            out_weight.reshape(n_zh, n_x, n_core, head_dim, feat), (2, 1, 0, 3, 4)
        ).reshape(-1, feat)
        partial = jnp.einsum(
            "tf,hf->th", grad_rows, weight_perm, preferred_element_type=jnp.float32
        ).astype(jnp.bfloat16)
        partial = pp_reduce_scatter_cols(partial, "core", n_core).astype(jnp.bfloat16)
        context, partial = lax.optimization_barrier((context, partial))
        ctx_all = lax.all_gather(context[None], ("zh", DEP, "x", "core"), axis=0, tiled=True)
        ctx_all = ctx_all.reshape(n_zh, n_dep, n_x, n_core, tok_depth, head_dim)
        partial = pp_reduce_scatter_cols(partial, "x", n_x).astype(jnp.bfloat16)
        partial = pp_reduce_scatter_cols(partial, "zh", n_zh).astype(jnp.bfloat16)
        context_grad = roll_rows(partial, me_r * n_tok, 0)

        grad_prob = jnp.dot(context_grad, values_all.T, preferred_element_type=jnp.float32)
        delta_row = jnp.sum(prob_full * grad_prob, axis=1, keepdims=True)
        grad_score = (prob_full * (grad_prob - delta_row)).astype(jnp.bfloat16)
        grad_query = (
            jnp.dot(grad_score, keys_all, preferred_element_type=jnp.float32) * inv_root
        ).astype(jnp.bfloat16)
        key_partial = (
            jnp.einsum("qk,qh->kh", grad_score, query_rows, preferred_element_type=jnp.float32)
            * inv_root
        ).astype(jnp.bfloat16)
        value_partial = jnp.einsum(
            "qk,qh->kh", prob_half, context_grad, preferred_element_type=jnp.float32
        ).astype(jnp.bfloat16)
        kv_partial = jnp.concatenate([key_partial, value_partial], axis=1).reshape(
            n_dep, tok_depth, 2 * head_dim
        )
        kv_grad = kv_partial[0].astype(jnp.float32)
        for s in range(1, n_dep):
            kv_grad = kv_grad + shift_open(kv_partial[s], DEP, n_dep, -s).astype(jnp.float32)
        kv_grad = kv_grad.astype(jnp.bfloat16)
        grad_key, grad_value = kv_grad[:, :head_dim], kv_grad[:, head_dim:]

        grad_weight = None
        for depth in range(n_dep):
            piece = jnp.einsum(
                "zxcth,tf->zxchf",
                ctx_all[:, depth],
                rows_all[depth].reshape(tok_depth, feat),
                preferred_element_type=jnp.float32,
            )
            grad_weight = piece if grad_weight is None else grad_weight + piece
            if depth < n_dep - 1:
                grad_weight = lax.optimization_barrier(grad_weight)
        grad_weight = grad_weight.reshape(n_zh * n_x * n_core * head_dim, feat)
        return (grad_weight, grad_query, grad_key, grad_value)

    return shards


def solution(mesh):
    n_row, n_col, n_dep = mesh.shape["row"], mesh.shape["col"], mesh.shape["dep"]
    n_zh, n_core = 2, 2
    n_x = n_col // (n_zh * n_core)
    fine = Mesh(
        mesh.devices.reshape(n_row, n_zh, n_x, n_core, n_dep), ("row",) + COL + (DEP,)
    )
    in_specs = (
        P("row", DEP, COL),
        P("row", COL),
        P(DEP, ("row",) + COL),
        P(DEP, ("row",) + COL),
        P(DEP, ("row",) + COL),
        P(),
    )
    out_specs = (
        P("row", COL),
        P(DEP, ("row",) + COL),
        P(DEP, ("row",) + COL),
        P(DEP, ("row",) + COL),
    )
    return jax.shard_map(
        make_shards(n_zh, n_x, n_core, n_row, n_dep),
        mesh=fine,
        in_specs=in_specs,
        out_specs=out_specs,
        check_vma=False,
    )
```

```python
import math

import jax
import jax.numpy as jnp
from jax import lax
from jax.sharding import Mesh
from jax.sharding import PartitionSpec as P

NEG_FILL = -1e30
FAR = 1 << 30
COL = ("zh", "x", "core")
DEP = "zl"


def segment_count(positions, seg_ends):
    return jnp.sum((positions[:, None] >= seg_ends[None, :]).astype(jnp.int32), axis=1)


def shift(x, axis, n, s):
    return lax.ppermute(x, axis, [(i, (i + s) % n) for i in range(n)])


def shift_open(x, axis, n, s):
    return lax.ppermute(x, axis, [(i, i + s) for i in range(n) if 0 <= i + s < n])


def roll_rows(x, amount, axis):
    size = x.shape[axis]
    doubled = jnp.concatenate([x, x], axis=axis)
    return lax.dynamic_slice_in_dim(doubled, (size - amount) % size, size, axis=axis)


def rolled_gather(x, axis, n, stack_axis=0):
    parts = [x] + [shift(x, axis, n, -s) for s in range(1, n)]
    return jnp.stack(parts, axis=stack_axis)


def pp_reduce_scatter(x, axis, n, dim):
    me = lax.axis_index(axis)
    acc = lax.dynamic_index_in_dim(x, me, dim, keepdims=False).astype(jnp.float32)
    for s in range(1, n):
        send = lax.dynamic_index_in_dim(x, (me + s) % n, dim, keepdims=False)
        acc = acc + shift(send, axis, n, s).astype(jnp.float32)
    return acc


def pp_reduce_scatter_cols(x, axis, n):
    me = lax.axis_index(axis)
    width = x.shape[1] // n
    acc = lax.dynamic_slice_in_dim(x, me * width, width, axis=1).astype(jnp.float32)
    for s in range(1, n):
        send = lax.dynamic_slice_in_dim(x, ((me + s) % n) * width, width, axis=1)
        acc = acc + shift(send, axis, n, s).astype(jnp.float32)
    return acc


def make_shards(n_zh, n_x, n_core, n_row, n_dep):
    def shards(grad_out, out_weight, query_rows, key_rows, value_rows, seg_lengths):
        n_tok, feat = grad_out.shape[1], grad_out.shape[2]
        tok_depth = n_row * n_tok
        head_dim = query_rows.shape[1]
        inv_root = 1.0 / math.sqrt(head_dim)
        me_r = lax.axis_index("row")
        me_d = lax.axis_index(DEP)
        local = grad_out[0]
        grad_rows = rolled_gather(local, "row", n_row).reshape(tok_depth, feat)

        kv = jnp.concatenate([key_rows, value_rows], axis=1)
        kv_all = jnp.stack(
            [kv] + [shift_open(kv, DEP, n_dep, t) for t in range(1, n_dep)], axis=0
        ).reshape(n_dep * tok_depth, 2 * head_dim)
        keys_all, values_all = kv_all[:, :head_dim], kv_all[:, head_dim:]
        by_depth = roll_rows(rolled_gather(local, DEP, n_dep), me_d, 0)

        src_depth = me_d - jnp.arange(n_dep, dtype=jnp.int32)
        key_pos = (
            jnp.where(src_depth >= 0, src_depth * tok_depth, FAR)[:, None]
            + jnp.arange(tok_depth, dtype=jnp.int32)[None, :]
        ).reshape(-1)
        seg_ends = jnp.cumsum(seg_lengths)
        key_seg = segment_count(key_pos, seg_ends)
        query_pos = me_d * tok_depth + jnp.arange(tok_depth, dtype=jnp.int32)
        query_seg = segment_count(query_pos, seg_ends)
        allowed = (query_seg[:, None] == key_seg[None, :]) & (
            key_pos[None, :] <= query_pos[:, None]
        )
        scores = (
            jnp.einsum("qh,kh->qk", query_rows, keys_all, preferred_element_type=jnp.float32)
            * inv_root
        )
        masked = jnp.where(allowed, scores, NEG_FILL)
        row_max = jnp.max(masked, axis=1, keepdims=True)
        exponent = jnp.where(allowed, jnp.exp(masked - row_max), 0.0)
        row_sum = jnp.sum(exponent, axis=1, keepdims=True)
        prob_full = exponent / row_sum
        prob_half = prob_full.astype(jnp.bfloat16)
        context = jnp.dot(prob_half, values_all, preferred_element_type=jnp.float32).astype(
            jnp.bfloat16
        )

        rows_all = rolled_gather(by_depth, "row", n_row, stack_axis=1)
        context = roll_rows(context, -me_r * n_tok, 0)

        weight_perm = jnp.transpose(
            out_weight.reshape(n_zh, n_x, n_core, head_dim, feat), (2, 1, 0, 3, 4)
        ).reshape(-1, feat)
        partial = jnp.einsum(
            "tf,hf->th", grad_rows, weight_perm, preferred_element_type=jnp.float32
        ).astype(jnp.bfloat16)
        partial = pp_reduce_scatter_cols(partial, "core", n_core).astype(jnp.bfloat16)
        context, partial, by_depth = lax.optimization_barrier((context, partial, by_depth))
        ctx_all = lax.all_gather(context[None], ("zh", DEP, "x", "core"), axis=0, tiled=True)
        ctx_all = ctx_all.reshape(n_zh, n_dep, n_x, n_core, tok_depth, head_dim)
        partial = pp_reduce_scatter_cols(partial, "x", n_x).astype(jnp.bfloat16)
        partial = pp_reduce_scatter_cols(partial, "zh", n_zh).astype(jnp.bfloat16)
        context_grad = roll_rows(partial, me_r * n_tok, 0)

        grad_prob = jnp.dot(context_grad, values_all.T, preferred_element_type=jnp.float32)
        delta_row = jnp.sum(prob_full * grad_prob, axis=1, keepdims=True)
        grad_score = (prob_full * (grad_prob - delta_row)).astype(jnp.bfloat16)
        grad_query = (
            jnp.dot(grad_score, keys_all, preferred_element_type=jnp.float32) * inv_root
        ).astype(jnp.bfloat16)
        key_partial = (
            jnp.einsum("qk,qh->kh", grad_score, query_rows, preferred_element_type=jnp.float32)
            * inv_root
        ).astype(jnp.bfloat16)
        value_partial = jnp.einsum(
            "qk,qh->kh", prob_half, context_grad, preferred_element_type=jnp.float32
        ).astype(jnp.bfloat16)
        kv_partial = jnp.concatenate([key_partial, value_partial], axis=1).reshape(
            n_dep, tok_depth, 2 * head_dim
        )
        kv_grad = kv_partial[0].astype(jnp.float32)
        for s in range(1, n_dep):
            kv_grad = kv_grad + shift_open(kv_partial[s], DEP, n_dep, -s).astype(jnp.float32)
        kv_grad = kv_grad.astype(jnp.bfloat16)
        grad_key, grad_value = kv_grad[:, :head_dim], kv_grad[:, head_dim:]

        grad_weight = None
        for depth in range(n_dep):
            piece = jnp.einsum(
                "zxcth,tf->zxchf",
                ctx_all[:, depth],
                rows_all[depth].reshape(tok_depth, feat),
                preferred_element_type=jnp.float32,
            )
            grad_weight = piece if grad_weight is None else grad_weight + piece
            if depth < n_dep - 1:
                grad_weight = lax.optimization_barrier(grad_weight)
        grad_weight = grad_weight.reshape(n_zh * n_x * n_core * head_dim, feat)
        return (grad_weight, grad_query, grad_key, grad_value)

    return shards


def solution(mesh):
    n_row, n_col, n_dep = mesh.shape["row"], mesh.shape["col"], mesh.shape["dep"]
    n_zh, n_core = 2, 2
    n_x = n_col // (n_zh * n_core)
    fine = Mesh(
        mesh.devices.reshape(n_row, n_zh, n_x, n_core, n_dep), ("row",) + COL + (DEP,)
    )
    in_specs = (
        P("row", DEP, COL),
        P("row", COL),
        P(DEP, ("row",) + COL),
        P(DEP, ("row",) + COL),
        P(DEP, ("row",) + COL),
        P(),
    )
    out_specs = (
        P("row", COL),
        P(DEP, ("row",) + COL),
        P(DEP, ("row",) + COL),
        P(DEP, ("row",) + COL),
    )
    return jax.shard_map(
        make_shards(n_zh, n_x, n_core, n_row, n_dep),
        mesh=fine,
        in_specs=in_specs,
        out_specs=out_specs,
        check_vma=False,
    )
```

```python
import math

import jax
import jax.numpy as jnp
from jax import lax
from jax.sharding import Mesh
from jax.sharding import PartitionSpec as P

NEG_FILL = -1e30
FAR = 1 << 30
COL = ("zh", "x", "core")
DEP = "zl"


def segment_count(positions, seg_ends):
    return jnp.sum((positions[:, None] >= seg_ends[None, :]).astype(jnp.int32), axis=1)


def shift(x, axis, n, s):
    return lax.ppermute(x, axis, [(i, (i + s) % n) for i in range(n)])


def shift_open(x, axis, n, s):
    return lax.ppermute(x, axis, [(i, i + s) for i in range(n) if 0 <= i + s < n])


def roll_rows(x, amount, axis):
    size = x.shape[axis]
    doubled = jnp.concatenate([x, x], axis=axis)
    return lax.dynamic_slice_in_dim(doubled, (size - amount) % size, size, axis=axis)


def rolled_gather(x, axis, n, stack_axis=0):
    parts = [x] + [shift(x, axis, n, -s) for s in range(1, n)]
    return jnp.stack(parts, axis=stack_axis)


def pp_reduce_scatter(x, axis, n, dim):
    me = lax.axis_index(axis)
    acc = lax.dynamic_index_in_dim(x, me, dim, keepdims=False).astype(jnp.float32)
    for s in range(1, n):
        send = lax.dynamic_index_in_dim(x, (me + s) % n, dim, keepdims=False)
        acc = acc + shift(send, axis, n, s).astype(jnp.float32)
    return acc


def pp_reduce_scatter_cols(x, axis, n):
    me = lax.axis_index(axis)
    width = x.shape[1] // n
    acc = lax.dynamic_slice_in_dim(x, me * width, width, axis=1).astype(jnp.float32)
    for s in range(1, n):
        send = lax.dynamic_slice_in_dim(x, ((me + s) % n) * width, width, axis=1)
        acc = acc + shift(send, axis, n, s).astype(jnp.float32)
    return acc


def make_shards(n_zh, n_x, n_core, n_row, n_dep):
    def shards(grad_out, out_weight, query_rows, key_rows, value_rows, seg_lengths):
        n_tok, feat = grad_out.shape[1], grad_out.shape[2]
        tok_depth = n_row * n_tok
        head_dim = query_rows.shape[1]
        inv_root = 1.0 / math.sqrt(head_dim)
        me_r = lax.axis_index("row")
        me_d = lax.axis_index(DEP)
        local = grad_out[0]
        grad_rows = rolled_gather(local, "row", n_row).reshape(tok_depth, feat)

        kv = jnp.concatenate([key_rows, value_rows], axis=1)
        kv_all = jnp.stack(
            [kv] + [shift_open(kv, DEP, n_dep, t) for t in range(1, n_dep)], axis=0
        ).reshape(n_dep * tok_depth, 2 * head_dim)
        keys_all, values_all = kv_all[:, :head_dim], kv_all[:, head_dim:]
        by_depth = roll_rows(rolled_gather(local, DEP, n_dep), me_d, 0)

        src_depth = me_d - jnp.arange(n_dep, dtype=jnp.int32)
        key_pos = (
            jnp.where(src_depth >= 0, src_depth * tok_depth, FAR)[:, None]
            + jnp.arange(tok_depth, dtype=jnp.int32)[None, :]
        ).reshape(-1)
        seg_ends = jnp.cumsum(seg_lengths)
        key_seg = segment_count(key_pos, seg_ends)
        query_rows = roll_rows(query_rows, -me_r * n_tok, 0)
        query_pos = me_d * tok_depth + (
            jnp.arange(tok_depth, dtype=jnp.int32) + me_r * n_tok
        ) % tok_depth
        query_seg = segment_count(query_pos, seg_ends)
        allowed = (query_seg[:, None] == key_seg[None, :]) & (
            key_pos[None, :] <= query_pos[:, None]
        )
        scores = (
            jnp.einsum("qh,kh->qk", query_rows, keys_all, preferred_element_type=jnp.float32)
            * inv_root
        )
        masked = jnp.where(allowed, scores, NEG_FILL)
        row_max = jnp.max(masked, axis=1, keepdims=True)
        exponent = jnp.where(allowed, jnp.exp(masked - row_max), 0.0)
        row_sum = jnp.sum(exponent, axis=1, keepdims=True)
        prob_full = exponent / row_sum
        prob_half = prob_full.astype(jnp.bfloat16)
        context = jnp.dot(prob_half, values_all, preferred_element_type=jnp.float32).astype(
            jnp.bfloat16
        )

        rows_all = rolled_gather(by_depth, "row", n_row, stack_axis=1)

        weight_perm = jnp.transpose(
            out_weight.reshape(n_zh, n_x, n_core, head_dim, feat), (2, 1, 0, 3, 4)
        ).reshape(-1, feat)
        partial = jnp.einsum(
            "tf,hf->th", grad_rows, weight_perm, preferred_element_type=jnp.float32
        ).astype(jnp.bfloat16)
        partial = pp_reduce_scatter_cols(partial, "core", n_core).astype(jnp.bfloat16)
        context, partial, by_depth = lax.optimization_barrier((context, partial, by_depth))
        ctx_all = lax.all_gather(context[None], ("zh", DEP, "x", "core"), axis=0, tiled=True)
        ctx_all = ctx_all.reshape(n_zh, n_dep, n_x, n_core, tok_depth, head_dim)
        partial = pp_reduce_scatter_cols(partial, "x", n_x).astype(jnp.bfloat16)
        partial = pp_reduce_scatter_cols(partial, "zh", n_zh).astype(jnp.bfloat16)
        context_grad = partial

        grad_prob = jnp.dot(context_grad, values_all.T, preferred_element_type=jnp.float32)
        delta_row = jnp.sum(prob_full * grad_prob, axis=1, keepdims=True)
        grad_score = (prob_full * (grad_prob - delta_row)).astype(jnp.bfloat16)
        grad_query = (
            jnp.dot(grad_score, keys_all, preferred_element_type=jnp.float32) * inv_root
        ).astype(jnp.bfloat16)
        key_partial = (
            jnp.einsum("qk,qh->kh", grad_score, query_rows, preferred_element_type=jnp.float32)
            * inv_root
        ).astype(jnp.bfloat16)
        value_partial = jnp.einsum(
            "qk,qh->kh", prob_half, context_grad, preferred_element_type=jnp.float32
        ).astype(jnp.bfloat16)
        kv_partial = jnp.concatenate([key_partial, value_partial], axis=1).reshape(
            n_dep, tok_depth, 2 * head_dim
        )
        kv_grad = kv_partial[0].astype(jnp.float32)
        for s in range(1, n_dep):
            kv_grad = kv_grad + shift_open(kv_partial[s], DEP, n_dep, -s).astype(jnp.float32)
        kv_grad = kv_grad.astype(jnp.bfloat16)
        grad_key, grad_value = kv_grad[:, :head_dim], kv_grad[:, head_dim:]

        grad_weight = None
        for depth in range(n_dep):
            piece = jnp.einsum(
                "zxcth,tf->zxchf",
                ctx_all[:, depth],
                rows_all[depth].reshape(tok_depth, feat),
                preferred_element_type=jnp.float32,
            )
            grad_weight = piece if grad_weight is None else grad_weight + piece
            if depth < n_dep - 1:
                grad_weight = lax.optimization_barrier(grad_weight)
        grad_weight = grad_weight.reshape(n_zh * n_x * n_core * head_dim, feat)
        grad_query = roll_rows(grad_query, me_r * n_tok, 0)
        return (grad_weight, grad_query, grad_key, grad_value)

    return shards


def solution(mesh):
    n_row, n_col, n_dep = mesh.shape["row"], mesh.shape["col"], mesh.shape["dep"]
    n_zh, n_core = 2, 2
    n_x = n_col // (n_zh * n_core)
    fine = Mesh(
        mesh.devices.reshape(n_row, n_zh, n_x, n_core, n_dep), ("row",) + COL + (DEP,)
    )
    in_specs = (
        P("row", DEP, COL),
        P("row", COL),
        P(DEP, ("row",) + COL),
        P(DEP, ("row",) + COL),
        P(DEP, ("row",) + COL),
        P(),
    )
    out_specs = (
        P("row", COL),
        P(DEP, ("row",) + COL),
        P(DEP, ("row",) + COL),
        P(DEP, ("row",) + COL),
    )
    return jax.shard_map(
        make_shards(n_zh, n_x, n_core, n_row, n_dep),
        mesh=fine,
        in_specs=in_specs,
        out_specs=out_specs,
        check_vma=False,
    )
```

```python
import math

import jax
import jax.numpy as jnp
from jax import lax
from jax.sharding import Mesh
from jax.sharding import PartitionSpec as P

NEG_FILL = -1e30
FAR = 1 << 30
COL = ("zh", "x", "core")
DEP = "zl"


def segment_count(positions, seg_ends):
    return jnp.sum((positions[:, None] >= seg_ends[None, :]).astype(jnp.int32), axis=1)


def shift(x, axis, n, s):
    return lax.ppermute(x, axis, [(i, (i + s) % n) for i in range(n)])


def shift_open(x, axis, n, s):
    return lax.ppermute(x, axis, [(i, i + s) for i in range(n) if 0 <= i + s < n])


def roll_rows(x, amount, axis):
    size = x.shape[axis]
    doubled = jnp.concatenate([x, x], axis=axis)
    return lax.dynamic_slice_in_dim(doubled, (size - amount) % size, size, axis=axis)


def rolled_gather(x, axis, n, stack_axis=0):
    parts = [x] + [shift(x, axis, n, -s) for s in range(1, n)]
    return jnp.stack(parts, axis=stack_axis)


def pp_reduce_scatter(x, axis, n, dim):
    me = lax.axis_index(axis)
    acc = lax.dynamic_index_in_dim(x, me, dim, keepdims=False).astype(jnp.float32)
    for s in range(1, n):
        send = lax.dynamic_index_in_dim(x, (me + s) % n, dim, keepdims=False)
        acc = acc + shift(send, axis, n, s).astype(jnp.float32)
    return acc


def pp_reduce_scatter_cols(x, axis, n):
    me = lax.axis_index(axis)
    width = x.shape[1] // n
    acc = lax.dynamic_slice_in_dim(x, me * width, width, axis=1).astype(jnp.float32)
    for s in range(1, n):
        send = lax.dynamic_slice_in_dim(x, ((me + s) % n) * width, width, axis=1)
        acc = acc + shift(send, axis, n, s).astype(jnp.float32)
    return acc


def make_shards(n_zh, n_x, n_core, n_row, n_dep):
    def shards(grad_out, out_weight, query_rows, key_rows, value_rows, seg_lengths):
        n_tok, feat = grad_out.shape[1], grad_out.shape[2]
        tok_depth = n_row * n_tok
        head_dim = query_rows.shape[1]
        inv_root = 1.0 / math.sqrt(head_dim)
        me_r = lax.axis_index("row")
        me_d = lax.axis_index(DEP)
        local = grad_out[0]
        grad_rows = rolled_gather(local, "row", n_row).reshape(tok_depth, feat)

        kv = jnp.concatenate([key_rows, value_rows], axis=1)
        kv_all = jnp.stack(
            [kv] + [shift_open(kv, DEP, n_dep, t) for t in range(1, n_dep)], axis=0
        ).reshape(n_dep * tok_depth, 2 * head_dim)
        keys_all, values_all = kv_all[:, :head_dim], kv_all[:, head_dim:]
        by_depth = roll_rows(rolled_gather(local, DEP, n_dep), me_d, 0)

        src_depth = me_d - jnp.arange(n_dep, dtype=jnp.int32)
        key_pos = (
            jnp.where(src_depth >= 0, src_depth * tok_depth, FAR)[:, None]
            + jnp.arange(tok_depth, dtype=jnp.int32)[None, :]
        ).reshape(-1)
        seg_ends = jnp.cumsum(seg_lengths)
        key_seg = segment_count(key_pos, seg_ends)
        query_rows = roll_rows(query_rows, -me_r * n_tok, 0)
        query_pos = me_d * tok_depth + (
            jnp.arange(tok_depth, dtype=jnp.int32) + me_r * n_tok
        ) % tok_depth
        query_seg = segment_count(query_pos, seg_ends)
        allowed = (query_seg[:, None] == key_seg[None, :]) & (
            key_pos[None, :] <= query_pos[:, None]
        )
        scores = (
            jnp.einsum("qh,kh->qk", query_rows, keys_all, preferred_element_type=jnp.float32)
            * inv_root
        )
        masked = jnp.where(allowed, scores, NEG_FILL)
        row_max = jnp.max(masked, axis=1, keepdims=True)
        exponent = jnp.where(allowed, jnp.exp(masked - row_max), 0.0)
        row_sum = jnp.sum(exponent, axis=1, keepdims=True)
        prob_full = exponent * (1.0 / row_sum)
        prob_half = prob_full.astype(jnp.bfloat16)
        context = jnp.dot(prob_half, values_all, preferred_element_type=jnp.float32).astype(
            jnp.bfloat16
        )

        rows_all = rolled_gather(by_depth, "row", n_row, stack_axis=1)

        weight_perm = jnp.transpose(
            out_weight.reshape(n_zh, n_x, n_core, head_dim, feat), (2, 1, 0, 3, 4)
        ).reshape(-1, feat)
        partial = jnp.einsum(
            "tf,hf->th", grad_rows, weight_perm, preferred_element_type=jnp.float32
        ).astype(jnp.bfloat16)
        partial = pp_reduce_scatter_cols(partial, "core", n_core).astype(jnp.bfloat16)
        context, partial, by_depth = lax.optimization_barrier((context, partial, by_depth))
        ctx_all = lax.all_gather(context[None], ("zh", DEP, "x", "core"), axis=0, tiled=True)
        ctx_all = ctx_all.reshape(n_zh, n_dep, n_x, n_core, tok_depth, head_dim)
        partial = pp_reduce_scatter_cols(partial, "x", n_x).astype(jnp.bfloat16)
        partial = pp_reduce_scatter_cols(partial, "zh", n_zh).astype(jnp.bfloat16)
        context_grad = partial

        grad_prob = jnp.dot(context_grad, values_all.T, preferred_element_type=jnp.float32)
        delta_row = jnp.sum(prob_full * grad_prob, axis=1, keepdims=True)
        grad_score = (prob_full * (grad_prob - delta_row)).astype(jnp.bfloat16)
        grad_query = (
            jnp.dot(grad_score, keys_all, preferred_element_type=jnp.float32) * inv_root
        ).astype(jnp.bfloat16)
        key_partial = (
            jnp.einsum("qk,qh->kh", grad_score, query_rows, preferred_element_type=jnp.float32)
            * inv_root
        ).astype(jnp.bfloat16)
        value_partial = jnp.einsum(
            "qk,qh->kh", prob_half, context_grad, preferred_element_type=jnp.float32
        ).astype(jnp.bfloat16)
        kv_partial = jnp.concatenate([key_partial, value_partial], axis=1).reshape(
            n_dep, tok_depth, 2 * head_dim
        )
        kv_grad = kv_partial[0].astype(jnp.float32)
        for s in range(1, n_dep):
            kv_grad = kv_grad + shift_open(kv_partial[s], DEP, n_dep, -s).astype(jnp.float32)
        kv_grad = kv_grad.astype(jnp.bfloat16)
        grad_key, grad_value = kv_grad[:, :head_dim], kv_grad[:, head_dim:]

        grad_weight = None
        for depth in range(n_dep):
            piece = jnp.einsum(
                "zxcth,tf->zxchf",
                ctx_all[:, depth],
                rows_all[depth].reshape(tok_depth, feat),
                preferred_element_type=jnp.float32,
            )
            grad_weight = piece if grad_weight is None else grad_weight + piece
            if depth < n_dep - 1:
                grad_weight = lax.optimization_barrier(grad_weight)
        grad_weight = grad_weight.reshape(n_zh * n_x * n_core * head_dim, feat)
        grad_query = roll_rows(grad_query, me_r * n_tok, 0)
        return (grad_weight, grad_query, grad_key, grad_value)

    return shards


def solution(mesh):
    n_row, n_col, n_dep = mesh.shape["row"], mesh.shape["col"], mesh.shape["dep"]
    n_zh, n_core = 2, 2
    n_x = n_col // (n_zh * n_core)
    fine = Mesh(
        mesh.devices.reshape(n_row, n_zh, n_x, n_core, n_dep), ("row",) + COL + (DEP,)
    )
    in_specs = (
        P("row", DEP, COL),
        P("row", COL),
        P(DEP, ("row",) + COL),
        P(DEP, ("row",) + COL),
        P(DEP, ("row",) + COL),
        P(),
    )
    out_specs = (
        P("row", COL),
        P(DEP, ("row",) + COL),
        P(DEP, ("row",) + COL),
        P(DEP, ("row",) + COL),
    )
    return jax.shard_map(
        make_shards(n_zh, n_x, n_core, n_row, n_dep),
        mesh=fine,
        in_specs=in_specs,
        out_specs=out_specs,
        check_vma=False,
    )
```

```python
import math

import jax
import jax.numpy as jnp
from jax import lax
from jax.sharding import Mesh
from jax.sharding import PartitionSpec as P

NEG_FILL = -1e30
FAR = 1 << 30
COL = ("zh", "x", "core")
DEP = "zl"


def segment_count(positions, seg_ends):
    return jnp.sum((positions[:, None] >= seg_ends[None, :]).astype(jnp.int32), axis=1)


def shift(x, axis, n, s):
    return lax.ppermute(x, axis, [(i, (i + s) % n) for i in range(n)])


def shift_open(x, axis, n, s):
    return lax.ppermute(x, axis, [(i, i + s) for i in range(n) if 0 <= i + s < n])


def roll_rows(x, amount, axis):
    size = x.shape[axis]
    doubled = jnp.concatenate([x, x], axis=axis)
    return lax.dynamic_slice_in_dim(doubled, (size - amount) % size, size, axis=axis)


def rolled_gather(x, axis, n, stack_axis=0):
    parts = [x] + [shift(x, axis, n, -s) for s in range(1, n)]
    return jnp.stack(parts, axis=stack_axis)


def pp_reduce_scatter(x, axis, n, dim):
    me = lax.axis_index(axis)
    acc = lax.dynamic_index_in_dim(x, me, dim, keepdims=False).astype(jnp.float32)
    for s in range(1, n):
        send = lax.dynamic_index_in_dim(x, (me + s) % n, dim, keepdims=False)
        acc = acc + shift(send, axis, n, s).astype(jnp.float32)
    return acc


def pp_reduce_scatter_cols(x, axis, n):
    me = lax.axis_index(axis)
    width = x.shape[1] // n
    acc = lax.dynamic_slice_in_dim(x, me * width, width, axis=1).astype(jnp.float32)
    for s in range(1, n):
        send = lax.dynamic_slice_in_dim(x, ((me + s) % n) * width, width, axis=1)
        acc = acc + shift(send, axis, n, s).astype(jnp.float32)
    return acc


def make_shards(n_zh, n_x, n_core, n_row, n_dep):
    def shards(grad_out, out_weight, query_rows, key_rows, value_rows, seg_lengths):
        n_tok, feat = grad_out.shape[1], grad_out.shape[2]
        tok_depth = n_row * n_tok
        head_dim = query_rows.shape[1]
        inv_root = 1.0 / math.sqrt(head_dim)
        me_r = lax.axis_index("row")
        me_d = lax.axis_index(DEP)
        local = grad_out[0]
        grad_rows = rolled_gather(local, "row", n_row).reshape(tok_depth, feat)

        kv = jnp.concatenate([key_rows, value_rows], axis=1)
        kv_all = jnp.stack(
            [kv] + [shift_open(kv, DEP, n_dep, t) for t in range(1, n_dep)], axis=0
        ).reshape(n_dep * tok_depth, 2 * head_dim)
        keys_all, values_all = kv_all[:, :head_dim], kv_all[:, head_dim:]
        by_depth = rolled_gather(local, DEP, n_dep)

        src_depth = me_d - jnp.arange(n_dep, dtype=jnp.int32)
        key_pos = (
            jnp.where(src_depth >= 0, src_depth * tok_depth, FAR)[:, None]
            + jnp.arange(tok_depth, dtype=jnp.int32)[None, :]
        ).reshape(-1)
        seg_ends = jnp.cumsum(seg_lengths)
        key_seg = segment_count(key_pos, seg_ends)
        query_rows = roll_rows(query_rows, -me_r * n_tok, 0)
        query_pos = me_d * tok_depth + (
            jnp.arange(tok_depth, dtype=jnp.int32) + me_r * n_tok
        ) % tok_depth
        query_seg = segment_count(query_pos, seg_ends)
        allowed = (query_seg[:, None] == key_seg[None, :]) & (
            key_pos[None, :] <= query_pos[:, None]
        )
        scores = (
            jnp.einsum("qh,kh->qk", query_rows, keys_all, preferred_element_type=jnp.float32)
            * inv_root
        )
        masked = jnp.where(allowed, scores, NEG_FILL)
        row_max = jnp.max(masked, axis=1, keepdims=True)
        exponent = jnp.where(allowed, jnp.exp(masked - row_max), 0.0)
        row_sum = jnp.sum(exponent, axis=1, keepdims=True)
        prob_full = exponent * (1.0 / row_sum)
        prob_half = prob_full.astype(jnp.bfloat16)
        context = jnp.dot(prob_half, values_all, preferred_element_type=jnp.float32).astype(
            jnp.bfloat16
        )


        weight_perm = jnp.transpose(
            out_weight.reshape(n_zh, n_x, n_core, head_dim, feat), (2, 1, 0, 3, 4)
        ).reshape(-1, feat)
        partial = jnp.einsum(
            "tf,hf->th", grad_rows, weight_perm, preferred_element_type=jnp.float32
        ).astype(jnp.bfloat16)
        partial = pp_reduce_scatter_cols(partial, "core", n_core).astype(jnp.bfloat16)
        context, partial, by_depth = lax.optimization_barrier((context, partial, by_depth))
        by_depth = roll_rows(by_depth, me_d, 0)
        rows_all = rolled_gather(by_depth, "row", n_row, stack_axis=1)
        ctx_all = lax.all_gather(context[None], ("zh", DEP, "x", "core"), axis=0, tiled=True)
        ctx_all = ctx_all.reshape(n_zh, n_dep, n_x, n_core, tok_depth, head_dim)
        partial = pp_reduce_scatter_cols(partial, "x", n_x).astype(jnp.bfloat16)
        partial = pp_reduce_scatter_cols(partial, "zh", n_zh).astype(jnp.bfloat16)
        context_grad = partial

        grad_prob = jnp.dot(context_grad, values_all.T, preferred_element_type=jnp.float32)
        delta_row = jnp.sum(prob_full * grad_prob, axis=1, keepdims=True)
        grad_score = (prob_full * (grad_prob - delta_row)).astype(jnp.bfloat16)
        grad_query = (
            jnp.dot(grad_score, keys_all, preferred_element_type=jnp.float32) * inv_root
        ).astype(jnp.bfloat16)
        key_partial = (
            jnp.einsum("qk,qh->kh", grad_score, query_rows, preferred_element_type=jnp.float32)
            * inv_root
        ).astype(jnp.bfloat16)
        value_partial = jnp.einsum(
            "qk,qh->kh", prob_half, context_grad, preferred_element_type=jnp.float32
        ).astype(jnp.bfloat16)
        kv_partial = jnp.concatenate([key_partial, value_partial], axis=1).reshape(
            n_dep, tok_depth, 2 * head_dim
        )
        kv_grad = kv_partial[0].astype(jnp.float32)
        for s in range(1, n_dep):
            kv_grad = kv_grad + shift_open(kv_partial[s], DEP, n_dep, -s).astype(jnp.float32)
        kv_grad = kv_grad.astype(jnp.bfloat16)
        grad_key, grad_value = kv_grad[:, :head_dim], kv_grad[:, head_dim:]

        grad_weight = None
        for depth in range(n_dep):
            piece = jnp.einsum(
                "zxcth,tf->zxchf",
                ctx_all[:, depth],
                rows_all[depth].reshape(tok_depth, feat),
                preferred_element_type=jnp.float32,
            )
            grad_weight = piece if grad_weight is None else grad_weight + piece
            if depth < n_dep - 1:
                grad_weight = lax.optimization_barrier(grad_weight)
        grad_weight = grad_weight.reshape(n_zh * n_x * n_core * head_dim, feat)
        grad_query = roll_rows(grad_query, me_r * n_tok, 0)
        return (grad_weight, grad_query, grad_key, grad_value)

    return shards


def solution(mesh):
    n_row, n_col, n_dep = mesh.shape["row"], mesh.shape["col"], mesh.shape["dep"]
    n_zh, n_core = 2, 2
    n_x = n_col // (n_zh * n_core)
    fine = Mesh(
        mesh.devices.reshape(n_row, n_zh, n_x, n_core, n_dep), ("row",) + COL + (DEP,)
    )
    in_specs = (
        P("row", DEP, COL),
        P("row", COL),
        P(DEP, ("row",) + COL),
        P(DEP, ("row",) + COL),
        P(DEP, ("row",) + COL),
        P(),
    )
    out_specs = (
        P("row", COL),
        P(DEP, ("row",) + COL),
        P(DEP, ("row",) + COL),
        P(DEP, ("row",) + COL),
    )
    return jax.shard_map(
        make_shards(n_zh, n_x, n_core, n_row, n_dep),
        mesh=fine,
        in_specs=in_specs,
        out_specs=out_specs,
        check_vma=False,
    )
```
